256 devices in a mesh: dp: 4 (over y), expert: 64 (over z, x, core).
Axes of the slice: x: 4, y: 4, z: 8, core: 2. Of those that a mesh axis runs over, the one named last changes fastest.
Arguments:
- hidden_states: bfloat16 [1024, 4, 4096], P('expert'), may hold values from -6 to 6
- routes: int32 [1024, 4, 8], P('expert'), may hold values from 0 to 63, all different within a row; in each aligned block of 64 rows (0 to 63, 64 to 127, ..., all dimensions but the last counted through in order) at most 16 rows name the same one
- route_weight: float32 [1024, 4, 8], P('expert'), may hold values from 0.05 to 1
- finish_step: int32 [1024], P('expert'), may hold values from 1 to 4
- group_keep: int32 [64], P('expert'), may hold values from 0 to 1
- dest_slot: int32 [1024], P('expert'), may hold values from 0 to 1023, as said below
- w_gate: bfloat16 [64, 4096, 1536], P('expert', None, 'dp'), may hold values from -0.09375 to 0.09375
- w_up: bfloat16 [64, 4096, 1536], P('expert', None, 'dp'), may hold values from -0.09375 to 0.09375
- w_down: bfloat16 [64, 1536, 4096], P('expert', 'dp'), may hold values from -0.15625 to 0.15625
Outputs:
- trainer_rows: bfloat16 [1024, 4, 4096], P(('dp', 'expert'))
The draws below stay inside these ranges and needn't reach their ends.
Inputs may be any that keep to these rules, and one draw needn't show every extreme that they name: `routes`: in the 64 row-steps of one prompt group (rows g * 16 to (g + 1) * 16 - 1, all steps), no expert is named more than 16 times, a bound that some block reaches; a row names 8 different experts at each step. dest_slot is a permutation of the slots; row r of group g = r // 16 goes to a slot (d * 64 + g) * 4 + i with 0 <= d < 4 and 0 <= i < 4.
All inputs are finite; a program needn't handle non-finite values.
Results may differ from the reference program's by a relative error of at most 0.0049.
Values may be sent and summed in bfloat16 or wider, within the bound.
No kernel may reach another device: no remote copies, remote signals or barrier semaphores. Data moves between devices by JAX's collectives and lax.ppermute only.
A program may use at most 128 MiB of HBM per device.

```python
import math
import jax
import jax.numpy as jnp
import numpy as np
from jax import lax

D = 4096
FF = 1536
TOP = 8
STEPS = 4
ROW_DEV = 16
EXPERTS = 64
ROWS = 1024
MOST = 16
SHARE = 4


def draw_dest_slot(key, part):
    group_total = ROWS // ROW_DEV
    group_keys = jax.random.split(jax.random.fold_in(key, 7), group_total)
    shuffled = jax.vmap(lambda one_key: jax.random.permutation(one_key, ROW_DEV))(group_keys)
    replica_of = shuffled // SHARE
    within = shuffled % SHARE
    group_index = jnp.arange(group_total, dtype=jnp.int32)[:, None]
    slots_out = (replica_of * group_total + group_index) * SHARE + within
    return slots_out.reshape(-1).astype(jnp.int32)


def draw_finish_step(key, part):
    first_key, second_key = jax.random.split(jax.random.fold_in(key, 11))
    codes = jax.random.randint(first_key, (ROWS,), 0, 20)
    table = jnp.array([4] * 16 + [1, 2, 3, 3], dtype=jnp.int32)
    values = table[codes]
    order = jax.random.permutation(second_key, ROWS)
    values = values.at[order[0]].set(1).at[order[1]].set(STEPS)
    return values.astype(jnp.int32)


def draw_group_keep(key, part):
    first_key, second_key = jax.random.split(jax.random.fold_in(key, 13))
    codes = jax.random.randint(first_key, (EXPERTS,), 0, 8)
    values = jnp.where(codes == 0, 0, 1).astype(jnp.int32)
    order = jax.random.permutation(second_key, EXPERTS)
    values = values.at[order[0]].set(0).at[order[1]].set(1)
    return values.astype(jnp.int32)


def steps_of(own_key, shape, shards, smallest, largest):
    def one(dim, shards_of):
        steps = jax.random.uniform(jax.random.fold_in(jax.random.fold_in(own_key, 6), dim), (shards_of,), jnp.float32, smallest / len(shards), largest / len(shards))
        return jnp.repeat(jnp.exp(steps), shape[dim] // shards_of).reshape((-1,) + (1,) * (len(shape) - dim - 1))

    level = one(*shards[0])
    for cut in shards[1:]:
        level = level * one(*cut)
    return level


def assign_block(own_key, own, number, rows, number_of, top, limit, lean):
    sequence = jax.random.permutation(own_key, number_of)
    packed, ordinary = portions_of(number_of, rows * top, limit, lean, True), portions_of(number_of, rows * top, limit, lean, False)
    places = jnp.arange(number_of)

    def named(sizes, turn):
        used = int((sizes > 0).sum())
        fixed = max(1, used // 4)
        passed = fixed + (places - fixed + turn * (used - fixed)) % max(1, number_of - fixed)
        return jnp.zeros((number_of,), jnp.int32).at[sequence[jnp.where(places < fixed, places, passed)]].set(jnp.asarray(sizes, jnp.int32))

    sizes = jnp.where(number % 4 == 0, named(packed, number // 4), named(ordinary, number - number // 4 - 1))
    mixed = jax.random.permutation(jax.random.fold_in(own, 3), number_of)
    source_of, receiver = mixed[0:number_of // 2 * 2:2], mixed[1:number_of // 2 * 2:2]
    room = jnp.minimum(sizes[source_of] - 1, limit - sizes[receiver]) // 2
    room = jnp.where((source_of == sequence[0]) | (receiver == sequence[0]) | (sizes[receiver] == 0), 0, jnp.maximum(room, 0))
    passed = jax.random.randint(jax.random.fold_in(own, 4), (number_of // 2,), 0, 1 << 20) % (room + 1)
    sizes = sizes.at[source_of].add(-passed).at[receiver].add(passed)
    labels = jnp.searchsorted(jnp.cumsum(sizes), jnp.arange(rows * top), side="right").astype(jnp.int32)
    table = labels.reshape(top, rows).T
    table = table[jax.random.permutation(jax.random.fold_in(own, 1), rows)]
    turn = jax.random.randint(jax.random.fold_in(own, 2), (rows, 1), 0, top)
    return jnp.take_along_axis(table, (jnp.arange(top)[None, :] + turn) % top, axis=1)


def portions_of(amount, total, reach, skew, full):
    portions = [(1 << 20) // math.isqrt(standing ** skew) + 1 for standing in range(1, amount + 1)]
    largest = reach if full else min(reach, max(-(-total // amount), total * portions[0] // sum(portions)))
    least = 1 if total - largest >= amount - 1 else 0
    given, rest = [largest] + [least] * (amount - 1), total - largest - least * (amount - 1)
    while rest > 0:
        movable = [i for i in range(1, amount) if given[i] < largest] or [i for i in range(1, amount) if given[i] < reach]
        mass, left = sum([portions[i] for i in movable]), rest
        for i in movable:
            addition = min(reach - given[i], max(1, left * portions[i] // mass), rest)
            given[i] = given[i] + addition
            rest = rest - addition
    return np.array(given)


def gaussian(key, extent, width, reach, shards=(), held_as=jnp.bfloat16):
    entries = jax.random.normal(key, extent, jnp.float32) * width
    if len(shards) > 0:
        entries = steps_of(key, extent, shards, -0.22, 0.18) * entries
    return jnp.clip(entries, min=-reach, max=reach).astype(held_as)


def setup_inputs(seed: int = 0) -> dict:
    splits = jax.random.split(jax.random.key(seed), 10)
    hidden_states = gaussian(splits[0], (ROWS, STEPS, D), 1.0, 6.0, ((0, 64),))
    routes_keys = jax.random.split(jax.random.fold_in(splits[1], 1), ROWS * STEPS // (ROW_DEV * STEPS))
    routes_turns = jax.random.permutation(jax.random.fold_in(splits[1], 3), ROWS * STEPS // (ROW_DEV * STEPS))
    routes = jax.vmap(lambda own, number: assign_block(jax.random.fold_in(splits[1], 2), own, number, ROW_DEV * STEPS, EXPERTS, TOP, MOST, 2))(routes_keys, routes_turns).reshape((ROWS, STEPS, TOP))
    route_weight = jnp.clip(jnp.exp(math.log(1.0) - 2.9957323 * jax.random.uniform(splits[2], (ROWS, STEPS, TOP), jnp.float32) ** steps_of(splits[2], (ROWS, STEPS, TOP), ((0, 64),), -0.2, 0.2)), 0.05, 1.0)
    finish_step = draw_finish_step(jax.random.fold_in(splits[9], 71), 0)
    group_keep = draw_group_keep(jax.random.fold_in(splits[9], 71), 0)
    dest_slot = draw_dest_slot(jax.random.fold_in(splits[9], 71), 0)
    w_gate = gaussian(splits[6], (EXPERTS, D, FF), D ** -0.5, 0.09375, ((0, 64), (2, 4)))
    w_up = gaussian(splits[7], (EXPERTS, D, FF), D ** -0.5, 0.09375, ((0, 64), (2, 4)))
    w_down = gaussian(splits[8], (EXPERTS, FF, D), FF ** -0.5, 0.15625, ((0, 64), (1, 4)))
    return dict(hidden_states=hidden_states, routes=routes, route_weight=route_weight, finish_step=finish_step, group_keep=group_keep, dest_slot=dest_slot, w_gate=w_gate, w_up=w_up, w_down=w_down)


def reference(hidden_states, routes, route_weight, finish_step, group_keep, dest_slot, w_gate, w_up, w_down):
    tokens = ROWS * STEPS
    capacity = MOST * (ROWS // ROW_DEV)
    step_ids = jnp.arange(STEPS, dtype=jnp.int32)
    keep_rows = jnp.repeat(group_keep, ROW_DEV)
    live_mask = ((step_ids[None, :] < finish_step[:, None]) & (keep_rows[:, None] == 1)).reshape(tokens)
    gate_share = route_weight / jnp.sum(route_weight, axis=2, keepdims=True)
    flat_inputs = hidden_states.reshape(tokens, D)
    flat_routes = routes.reshape(tokens, TOP)
    flat_share = gate_share.reshape(tokens, TOP)

    def per_expert(running, expert):
        picked = (flat_routes == expert) & live_mask[:, None]
        weight = jnp.sum(jnp.where(picked, flat_share, jnp.zeros_like(flat_share)), axis=1)
        hit_mask = jnp.any(picked, axis=1)
        picked_rows = jnp.nonzero(hit_mask, size=capacity, fill_value=0)[0].astype(jnp.int32)
        filled = jnp.arange(capacity, dtype=jnp.int32) < jnp.sum(hit_mask.astype(jnp.int32))
        rows_in = flat_inputs[picked_rows].astype(jnp.float32)
        gate_part = jnp.dot(rows_in, w_gate[expert].astype(jnp.float32), precision=lax.Precision.HIGHEST)
        up_part = jnp.dot(rows_in, w_up[expert].astype(jnp.float32), precision=lax.Precision.HIGHEST)
        activated = (jax.nn.silu(gate_part) * up_part).astype(jnp.bfloat16)
        expert_result = jnp.dot(activated.astype(jnp.float32), w_down[expert].astype(jnp.float32), precision=lax.Precision.HIGHEST)
        scale = jnp.where(filled, weight[picked_rows], jnp.zeros_like(weight[picked_rows]))
        running = running.at[picked_rows].add(scale[:, None] * expert_result)
        return running, None

    start = jnp.zeros((tokens, D), jnp.float32)
    combined, _ = lax.scan(per_expert, start, jnp.arange(EXPERTS, dtype=jnp.int32))
    combined = combined.reshape(ROWS, STEPS, D).astype(jnp.bfloat16)
    trainer_rows = jnp.zeros((ROWS, STEPS, D), jnp.bfloat16).at[dest_slot].set(combined)
    return trainer_rows
```

```python
import jax
import jax.numpy as jnp
from jax import lax
from jax.sharding import PartitionSpec as P

MOST_BASE = 16


def body(
    hidden_states, routes, route_weight, finish_step, group_keep, dest_slot, w_gate, w_up, w_down
):
    expert_count = lax.axis_size("expert")
    replica_count = lax.axis_size("dp")
    replica = lax.axis_index("dp")
    row_count, step_count, model_width = hidden_states.shape
    top_count = routes.shape[2]
    tokens = row_count * step_count
    slot_count = min(tokens, max(MOST_BASE, 2 * tokens * top_count // expert_count))
    slot_count = -(-slot_count // replica_count) * replica_count
    part = slot_count // replica_count
    step_ids = lax.broadcasted_iota(jnp.int32, (row_count, step_count), 1)
    live_mask = ((step_ids < finish_step[:, None]) & (group_keep[0] == 1)).reshape(tokens)
    gate_share = route_weight / jnp.sum(route_weight, axis=2, keepdims=True)
    expert_ids = lax.broadcasted_iota(jnp.int32, (1, 1, expert_count), 2)
    picked = (routes.reshape(tokens, top_count, 1) == expert_ids) & live_mask[:, None, None]
    hit_mask = jnp.sum(picked.astype(jnp.int32), axis=1)
    share_wide = jnp.broadcast_to(gate_share.reshape(tokens, top_count, 1), picked.shape)
    weight = jnp.sum(jnp.where(picked, share_wide, jnp.zeros_like(share_wide)), axis=1)
    prior_hits = jnp.cumsum(hit_mask, axis=0) - hit_mask
    slot_ids = replica * part + lax.broadcasted_iota(jnp.int32, (1, 1, part), 2)
    placement = (hit_mask[:, :, None] == 1) & (prior_hits[:, :, None] == slot_ids)
    weighted_place = (placement.astype(jnp.float32) * weight[:, :, None]).reshape(
        tokens, expert_count * part
    )
    placement = placement.reshape(tokens, expert_count * part)
    flat_inputs = hidden_states.reshape(tokens, model_width)
    outgoing = lax.dot_general(
        placement.astype(jnp.bfloat16),
        flat_inputs,
        (((0,), (0,)), ((), ())),
        preferred_element_type=jnp.float32,
    ).astype(jnp.bfloat16)
    outgoing = outgoing.reshape(expert_count, part, model_width)
    arrived = lax.all_to_all(outgoing, "expert", split_axis=0, concat_axis=0, tiled=True)
    gathered = lax.all_gather(arrived, "dp", axis=0, tiled=False)
    flattened = gathered.reshape(replica_count * expert_count * part, model_width)
    gate_part = jnp.dot(flattened, w_gate[0], preferred_element_type=jnp.float32)
    up_part = jnp.dot(flattened, w_up[0], preferred_element_type=jnp.float32)
    activated = (jax.nn.silu(gate_part) * up_part).astype(jnp.bfloat16)
    expert_result = jnp.dot(activated, w_down[0], preferred_element_type=jnp.float32)
    partial_out = expert_result.reshape(replica_count, expert_count, part, model_width)
    reduced = lax.psum_scatter(
        partial_out.astype(jnp.bfloat16), "dp", scatter_dimension=0, tiled=True
    )
    reduced = reduced.reshape(expert_count, part, model_width)
    returned_rows = lax.all_to_all(reduced, "expert", split_axis=0, concat_axis=0, tiled=True)
    share_rows = row_count // replica_count
    flat_device = dest_slot // share_rows
    target = flat_device // expert_count * share_rows + dest_slot % share_rows
    position_ids = lax.broadcasted_iota(jnp.int32, (replica_count * share_rows, row_count), 0)
    arrangement = (target[None, :] == position_ids).astype(jnp.float32)
    combined = jnp.dot(
        weighted_place,
        returned_rows.reshape(expert_count * part, model_width).astype(jnp.float32),
        precision=lax.Precision.HIGHEST,
        preferred_element_type=jnp.float32,
    )
    arranged = jnp.dot(
        arrangement,
        combined.reshape(row_count, step_count * model_width),
        precision=lax.Precision.HIGHEST,
        preferred_element_type=jnp.float32,
    )
    arranged = arranged.reshape(replica_count, share_rows, step_count, model_width)
    summed = lax.psum_scatter(arranged, "dp", scatter_dimension=0, tiled=True)
    return summed.reshape(share_rows, step_count, model_width).astype(jnp.bfloat16)


def solution(mesh):
    in_specs = (
        P("expert", None, None),
        P("expert", None, None),
        P("expert", None, None),
        P("expert"),
        P("expert"),
        P("expert"),
        P("expert", None, "dp"),
        P("expert", None, "dp"),
        P("expert", "dp", None),
    )
    out_specs = P(("dp", "expert"), None, None)
    return jax.shard_map(body, mesh=mesh, in_specs=in_specs, out_specs=out_specs, check_vma=False)
```

```python
import jax
import jax.numpy as jnp
from jax import lax
from jax.sharding import PartitionSpec as P

MOST_BASE = 16


def body(
    hidden_states, routes, route_weight, finish_step, group_keep, dest_slot, w_gate, w_up, w_down
):
    expert_count = lax.axis_size("expert")
    replica_count = lax.axis_size("dp")
    replica = lax.axis_index("dp")
    row_count, step_count, model_width = hidden_states.shape
    top_count = routes.shape[2]
    tokens = row_count * step_count
    slot_count = min(tokens, max(MOST_BASE, 2 * tokens * top_count // expert_count))
    slot_count = -(-slot_count // replica_count) * replica_count
    part = slot_count // replica_count
    step_ids = lax.broadcasted_iota(jnp.int32, (row_count, step_count), 1)
    live_mask = ((step_ids < finish_step[:, None]) & (group_keep[0] == 1)).reshape(tokens)
    gate_share = route_weight / jnp.sum(route_weight, axis=2, keepdims=True)
    expert_ids = lax.broadcasted_iota(jnp.int32, (1, 1, expert_count), 2)
    picked = (routes.reshape(tokens, top_count, 1) == expert_ids) & live_mask[:, None, None]
    hit_mask = jnp.sum(picked.astype(jnp.int32), axis=1)
    share_wide = jnp.broadcast_to(gate_share.reshape(tokens, top_count, 1), picked.shape)
    weight = jnp.sum(jnp.where(picked, share_wide, jnp.zeros_like(share_wide)), axis=1)
    prior_hits = jnp.cumsum(hit_mask, axis=0) - hit_mask
    flat_inputs = hidden_states.reshape(tokens, model_width)
    chunks = 2 if part % 2 == 0 else 1
    sub = part // chunks
    combined = jnp.zeros((tokens, model_width), jnp.float32)
    for chunk in range(chunks):
        first = replica * part + chunk * sub
        slot_ids = first + lax.broadcasted_iota(jnp.int32, (1, 1, sub), 2)
        placement = (hit_mask[:, :, None] == 1) & (prior_hits[:, :, None] == slot_ids)
        weighted_place = (placement.astype(jnp.float32) * weight[:, :, None]).reshape(
            tokens, expert_count * sub
        )
        placement = placement.reshape(tokens, expert_count * sub)
        outgoing = lax.dot_general(
            placement.astype(jnp.bfloat16),
            flat_inputs,
            (((0,), (0,)), ((), ())),
            preferred_element_type=jnp.float32,
        ).astype(jnp.bfloat16)
        arrived = lax.all_to_all(outgoing, "expert", split_axis=0, concat_axis=0, tiled=True)
        gathered = lax.all_gather(arrived, "dp", axis=0, tiled=True)
        gate_part = jnp.dot(gathered, w_gate[0], preferred_element_type=jnp.float32)
        up_part = jnp.dot(gathered, w_up[0], preferred_element_type=jnp.float32)
        activated = (jax.nn.silu(gate_part) * up_part).astype(jnp.bfloat16)
        expert_result = jnp.dot(activated, w_down[0], preferred_element_type=jnp.float32)
        reduced = lax.psum_scatter(
            expert_result.astype(jnp.bfloat16), "dp", scatter_dimension=0, tiled=True
        )
        returned_rows = lax.all_to_all(reduced, "expert", split_axis=0, concat_axis=0, tiled=True)
        combined = combined + jnp.dot(
            weighted_place,
            returned_rows.astype(jnp.float32),
            precision=lax.Precision.HIGHEST,
            preferred_element_type=jnp.float32,
        )
    share_rows = row_count // replica_count
    flat_device = dest_slot // share_rows
    target = flat_device // expert_count * share_rows + dest_slot % share_rows
    position_ids = lax.broadcasted_iota(jnp.int32, (replica_count * share_rows, row_count), 0)
    arrangement = (target[None, :] == position_ids).astype(jnp.float32)
    arranged = jnp.dot(
        arrangement,
        combined.reshape(row_count, step_count * model_width),
        precision=lax.Precision.HIGHEST,
        preferred_element_type=jnp.float32,
    )
    arranged = arranged.reshape(replica_count, share_rows, step_count, model_width)
    summed = lax.psum_scatter(arranged, "dp", scatter_dimension=0, tiled=True)
    summed = summed.reshape(share_rows, step_count, model_width)
    live_rows = live_mask.reshape(row_count, step_count).astype(jnp.float32)
    live_arranged = jnp.dot(arrangement, live_rows, precision=lax.Precision.HIGHEST)
    live_mine = lax.dynamic_slice_in_dim(live_arranged, replica * share_rows, share_rows, 0)
    summed = summed * live_mine[:, :, None]
    return summed.astype(jnp.bfloat16)


def solution(mesh):
    in_specs = (
        P("expert", None, None),
        P("expert", None, None),
        P("expert", None, None),
        P("expert"),
        P("expert"),
        P("expert"),
        P("expert", None, "dp"),
        P("expert", None, "dp"),
        P("expert", "dp", None),
    )
    out_specs = P(("dp", "expert"), None, None)
    return jax.shard_map(body, mesh=mesh, in_specs=in_specs, out_specs=out_specs, check_vma=False)
```

```python
import jax
import jax.numpy as jnp
from jax import lax
from jax.sharding import PartitionSpec as P

MOST_BASE = 16


def body(
    hidden_states, routes, route_weight, finish_step, group_keep, dest_slot, w_gate, w_up, w_down
):
    expert_count = lax.axis_size("expert")
    replica_count = lax.axis_size("dp")
    replica = lax.axis_index("dp")
    row_count, step_count, model_width = hidden_states.shape
    top_count = routes.shape[2]
    tokens = row_count * step_count
    slot_count = min(tokens, max(MOST_BASE, 2 * tokens * top_count // expert_count))
    slot_count = -(-slot_count // replica_count) * replica_count
    part = slot_count // replica_count
    step_ids = lax.broadcasted_iota(jnp.int32, (row_count, step_count), 1)
    live_mask = ((step_ids < finish_step[:, None]) & (group_keep[0] == 1)).reshape(tokens)
    gate_share = route_weight / jnp.sum(route_weight, axis=2, keepdims=True)
    expert_ids = lax.broadcasted_iota(jnp.int32, (1, 1, expert_count), 2)
    picked = (routes.reshape(tokens, top_count, 1) == expert_ids) & live_mask[:, None, None]
    hit_mask = jnp.sum(picked.astype(jnp.int32), axis=1)
    share_wide = jnp.broadcast_to(gate_share.reshape(tokens, top_count, 1), picked.shape)
    weight = jnp.sum(jnp.where(picked, share_wide, jnp.zeros_like(share_wide)), axis=1)
    prior_hits = jnp.cumsum(hit_mask, axis=0) - hit_mask
    flat_inputs = hidden_states.reshape(tokens, model_width)
    chunks = 2 if part % 2 == 0 else 1
    sub = part // chunks
    combined = jnp.zeros((tokens, model_width), jnp.float32)
    for chunk in range(chunks):
        first = replica * part + chunk * sub
        slot_ids = first + lax.broadcasted_iota(jnp.int32, (1, 1, sub), 2)
        placement = (hit_mask[:, :, None] == 1) & (prior_hits[:, :, None] == slot_ids)
        weighted_place = (placement.astype(jnp.float32) * weight[:, :, None]).reshape(
            tokens, expert_count * sub
        )
        placement = placement.reshape(tokens, expert_count * sub)
        outgoing = lax.dot_general(
            placement.astype(jnp.bfloat16),
            flat_inputs,
            (((0,), (0,)), ((), ())),
            preferred_element_type=jnp.float32,
        ).astype(jnp.bfloat16)
        arrived = lax.all_to_all(outgoing, "expert", split_axis=0, concat_axis=0, tiled=True)
        gathered = lax.all_gather(arrived, "dp", axis=0, tiled=True)
        gate_part = jnp.dot(gathered, w_gate[0], preferred_element_type=jnp.float32)
        up_part = jnp.dot(gathered, w_up[0], preferred_element_type=jnp.float32)
        activated = (jax.nn.silu(gate_part) * up_part).astype(jnp.bfloat16)
        expert_result = jnp.dot(activated, w_down[0], preferred_element_type=jnp.float32)
        quarters = lax.all_to_all(
            expert_result.astype(jnp.bfloat16), "dp", split_axis=0, concat_axis=0, tiled=True
        )
        reduced = jnp.sum(
            quarters.reshape(replica_count, expert_count * sub, model_width).astype(jnp.float32),
            axis=0,
        ).astype(jnp.bfloat16)
        returned_rows = lax.all_to_all(reduced, "expert", split_axis=0, concat_axis=0, tiled=True)
        combined = combined + jnp.dot(
            weighted_place,
            returned_rows.astype(jnp.float32),
            precision=lax.Precision.HIGHEST,
            preferred_element_type=jnp.float32,
        )
    share_rows = row_count // replica_count
    flat_device = dest_slot // share_rows
    target = flat_device // expert_count * share_rows + dest_slot % share_rows
    position_ids = lax.broadcasted_iota(jnp.int32, (replica_count * share_rows, row_count), 0)
    arrangement = (target[None, :] == position_ids).astype(jnp.float32)
    arranged = jnp.dot(
        arrangement,
        combined.reshape(row_count, step_count * model_width),
        precision=lax.Precision.HIGHEST,
        preferred_element_type=jnp.float32,
    )
    arranged = arranged.reshape(replica_count, share_rows, step_count, model_width)
    summed = jnp.sum(lax.all_to_all(arranged, "dp", split_axis=0, concat_axis=0, tiled=True), axis=0)
    live_rows = live_mask.reshape(row_count, step_count).astype(jnp.float32)
    live_arranged = jnp.dot(arrangement, live_rows, precision=lax.Precision.HIGHEST)
    live_mine = lax.dynamic_slice_in_dim(live_arranged, replica * share_rows, share_rows, 0)
    summed = summed * live_mine[:, :, None]
    return summed.astype(jnp.bfloat16)


def solution(mesh):
    in_specs = (
        P("expert", None, None),
        P("expert", None, None),
        P("expert", None, None),
        P("expert"),
        P("expert"),
        P("expert"),
        P("expert", None, "dp"),
        P("expert", None, "dp"),
        P("expert", "dp", None),
    )
    out_specs = P(("dp", "expert"), None, None)
    return jax.shard_map(body, mesh=mesh, in_specs=in_specs, out_specs=out_specs, check_vma=False)
```

```python
import jax
import jax.numpy as jnp
from jax import lax
from jax.sharding import PartitionSpec as P

MOST_BASE = 16


def exchange_sum(blocks, replica, replica_count):
    total = lax.dynamic_index_in_dim(blocks, replica, 0, keepdims=False).astype(jnp.float32)
    for shift in range(1, replica_count):
        outgoing = lax.dynamic_index_in_dim(
            blocks, (replica + shift) % replica_count, 0, keepdims=False
        )
        pairs = [(i, (i + shift) % replica_count) for i in range(replica_count)]
        total = total + lax.ppermute(outgoing, "dp", pairs).astype(jnp.float32)
    return total


def body(
    hidden_states, routes, route_weight, finish_step, group_keep, dest_slot, w_gate, w_up, w_down
):
    expert_count = lax.axis_size("expert")
    replica_count = lax.axis_size("dp")
    replica = lax.axis_index("dp")
    row_count, step_count, model_width = hidden_states.shape
    top_count = routes.shape[2]
    tokens = row_count * step_count
    slot_count = min(tokens, max(MOST_BASE, 2 * tokens * top_count // expert_count))
    slot_count = -(-slot_count // replica_count) * replica_count
    part = slot_count // replica_count
    step_ids = lax.broadcasted_iota(jnp.int32, (row_count, step_count), 1)
    live_mask = ((step_ids < finish_step[:, None]) & (group_keep[0] == 1)).reshape(tokens)
    gate_share = route_weight / jnp.sum(route_weight, axis=2, keepdims=True)
    expert_ids = lax.broadcasted_iota(jnp.int32, (1, 1, expert_count), 2)
    picked = (routes.reshape(tokens, top_count, 1) == expert_ids) & live_mask[:, None, None]
    hit_mask = jnp.sum(picked.astype(jnp.int32), axis=1)
    share_wide = jnp.broadcast_to(gate_share.reshape(tokens, top_count, 1), picked.shape)
    weight = jnp.sum(jnp.where(picked, share_wide, jnp.zeros_like(share_wide)), axis=1)
    prior_hits = jnp.cumsum(hit_mask, axis=0) - hit_mask
    flat_inputs = hidden_states.reshape(tokens, model_width)
    chunks = 2 if part % 2 == 0 else 1
    sub = part // chunks
    combined = jnp.zeros((tokens, model_width), jnp.float32)
    for chunk in range(chunks):
        first = replica * part + chunk * sub
        slot_ids = first + lax.broadcasted_iota(jnp.int32, (1, 1, sub), 2)
        placement = (hit_mask[:, :, None] == 1) & (prior_hits[:, :, None] == slot_ids)
        weighted_place = (placement.astype(jnp.float32) * weight[:, :, None]).reshape(
            tokens, expert_count * sub
        )
        placement = placement.reshape(tokens, expert_count * sub)
        outgoing = lax.dot_general(
            placement.astype(jnp.bfloat16),
            flat_inputs,
            (((0,), (0,)), ((), ())),
            preferred_element_type=jnp.float32,
        ).astype(jnp.bfloat16)
        arrived = lax.all_to_all(outgoing, "expert", split_axis=0, concat_axis=0, tiled=True)
        gathered = lax.all_gather(arrived, "dp", axis=0, tiled=True)
        gate_part = jnp.dot(gathered, w_gate[0], preferred_element_type=jnp.float32)
        up_part = jnp.dot(gathered, w_up[0], preferred_element_type=jnp.float32)
        activated = (jax.nn.silu(gate_part) * up_part).astype(jnp.bfloat16)
        expert_result = jnp.dot(activated, w_down[0], preferred_element_type=jnp.float32)
        blocks = expert_result.astype(jnp.bfloat16).reshape(
            replica_count, expert_count * sub, model_width
        )
        reduced = exchange_sum(blocks, replica, replica_count).astype(jnp.bfloat16)
        returned_rows = lax.all_to_all(reduced, "expert", split_axis=0, concat_axis=0, tiled=True)
        combined = combined + jnp.dot(
            weighted_place,
            returned_rows.astype(jnp.float32),
            precision=lax.Precision.HIGHEST,
            preferred_element_type=jnp.float32,
        )
    share_rows = row_count // replica_count
    flat_device = dest_slot // share_rows
    target = flat_device // expert_count * share_rows + dest_slot % share_rows
    position_ids = lax.broadcasted_iota(jnp.int32, (replica_count * share_rows, row_count), 0)
    arrangement = (target[None, :] == position_ids).astype(jnp.float32)
    arranged = jnp.dot(
        arrangement,
        combined.reshape(row_count, step_count * model_width),
        precision=lax.Precision.HIGHEST,
        preferred_element_type=jnp.float32,
    )
    arranged = arranged.reshape(replica_count, share_rows, step_count, model_width)
    summed = exchange_sum(arranged, replica, replica_count)
    live_rows = live_mask.reshape(row_count, step_count).astype(jnp.float32)
    live_arranged = jnp.dot(arrangement, live_rows, precision=lax.Precision.HIGHEST)
    live_mine = lax.dynamic_slice_in_dim(live_arranged, replica * share_rows, share_rows, 0)
    summed = summed * live_mine[:, :, None]
    return summed.astype(jnp.bfloat16)


def solution(mesh):
    in_specs = (
        P("expert", None, None),
        P("expert", None, None),
        P("expert", None, None),
        P("expert"),
        P("expert"),
        P("expert"),
        P("expert", None, "dp"),
        P("expert", None, "dp"),
        P("expert", "dp", None),
    )
    out_specs = P(("dp", "expert"), None, None)
    return jax.shard_map(body, mesh=mesh, in_specs=in_specs, out_specs=out_specs, check_vma=False)
```

```python
import jax
import jax.numpy as jnp
from jax import lax
from jax.sharding import PartitionSpec as P

MOST_BASE = 16


def exchange_gather(blocks, replica, replica_count):
    pieces = [None] * replica_count
    pieces[0] = lax.dynamic_index_in_dim(blocks, replica, 0, keepdims=False)
    for shift in range(1, replica_count):
        outgoing = lax.dynamic_index_in_dim(
            blocks, (replica + shift) % replica_count, 0, keepdims=False
        )
        pairs = [(i, (i + shift) % replica_count) for i in range(replica_count)]
        pieces[shift] = lax.ppermute(outgoing, "dp", pairs)
    stacked = jnp.stack(pieces, axis=0)
    order = (replica - lax.broadcasted_iota(jnp.int32, (replica_count,), 0)) % replica_count
    return jnp.take(stacked, order, axis=0)


def body(
    hidden_states, routes, route_weight, finish_step, group_keep, dest_slot, w_gate, w_up, w_down
):
    expert_count = lax.axis_size("expert")
    replica_count = lax.axis_size("dp")
    replica = lax.axis_index("dp")
    row_count, step_count, model_width = hidden_states.shape
    top_count = routes.shape[2]
    hidden_part = w_down.shape[1]
    columns = model_width // replica_count
    tokens = row_count * step_count
    slot_count = min(tokens, max(MOST_BASE, 2 * tokens * top_count // expert_count))
    slot_count = -(-slot_count // replica_count) * replica_count
    part = slot_count // replica_count
    down_blocks = w_down[0].reshape(hidden_part, replica_count, columns).transpose(1, 0, 2)
    down_cols = exchange_gather(down_blocks, replica, replica_count)
    step_ids = lax.broadcasted_iota(jnp.int32, (row_count, step_count), 1)
    live_mask = ((step_ids < finish_step[:, None]) & (group_keep[0] == 1)).reshape(tokens)
    gate_share = route_weight / jnp.sum(route_weight, axis=2, keepdims=True)
    expert_ids = lax.broadcasted_iota(jnp.int32, (1, 1, expert_count), 2)
    picked = (routes.reshape(tokens, top_count, 1) == expert_ids) & live_mask[:, None, None]
    hit_mask = jnp.sum(picked.astype(jnp.int32), axis=1)
    share_wide = jnp.broadcast_to(gate_share.reshape(tokens, top_count, 1), picked.shape)
    weight = jnp.sum(jnp.where(picked, share_wide, jnp.zeros_like(share_wide)), axis=1)
    prior_hits = jnp.cumsum(hit_mask, axis=0) - hit_mask
    flat_inputs = hidden_states.reshape(tokens, model_width)
    chunks = 2 if part % 2 == 0 else 1
    sub = part // chunks
    member_ids = lax.broadcasted_iota(jnp.int32, (1, 1, replica_count, 1), 2)
    within_ids = lax.broadcasted_iota(jnp.int32, (1, 1, 1, sub), 3)
    combined = jnp.zeros((tokens, columns), jnp.float32)
    for chunk in range(chunks):
        slot_ids = replica * part + chunk * sub + lax.broadcasted_iota(jnp.int32, (1, 1, sub), 2)
        placement = (hit_mask[:, :, None] == 1) & (prior_hits[:, :, None] == slot_ids)
        placement = placement.reshape(tokens, expert_count * sub)
        outgoing = lax.dot_general(
            placement.astype(jnp.bfloat16),
            flat_inputs,
            (((0,), (0,)), ((), ())),
            preferred_element_type=jnp.float32,
        ).astype(jnp.bfloat16)
        arrived = lax.all_to_all(outgoing, "expert", split_axis=0, concat_axis=0, tiled=True)
        gathered = lax.all_gather(arrived, "dp", axis=0, tiled=True)
        gate_part = jnp.dot(gathered, w_gate[0], preferred_element_type=jnp.float32)
        up_part = jnp.dot(gathered, w_up[0], preferred_element_type=jnp.float32)
        activated = (jax.nn.silu(gate_part) * up_part).astype(jnp.bfloat16)
        hidden_all = lax.all_gather(activated, "dp", axis=0, tiled=False)
        expert_cols = lax.dot_general(
            hidden_all,
            down_cols,
            (((0, 2), (0, 1)), ((), ())),
            preferred_element_type=jnp.float32,
        ).astype(jnp.bfloat16)
        by_source = expert_cols.reshape(replica_count, expert_count, sub, columns).transpose(
            1, 0, 2, 3
        )
        returned_rows = lax.all_to_all(by_source, "expert", split_axis=0, concat_axis=0, tiled=True)
        all_slot_ids = member_ids * part + chunk * sub + within_ids
        weighted_place = jnp.where(
            (hit_mask[:, :, None, None] == 1) & (prior_hits[:, :, None, None] == all_slot_ids),
            weight[:, :, None, None],
            0.0,
        ).reshape(tokens, expert_count * replica_count * sub)
        combined = combined + jnp.dot(
            weighted_place,
            returned_rows.reshape(expert_count * replica_count * sub, columns).astype(jnp.float32),
            precision=lax.Precision.HIGHEST,
            preferred_element_type=jnp.float32,
        )
    share_rows = row_count // replica_count
    flat_device = dest_slot // share_rows
    target = flat_device // expert_count * share_rows + dest_slot % share_rows
    position_ids = lax.broadcasted_iota(jnp.int32, (replica_count * share_rows, row_count), 0)
    arrangement = (target[None, :] == position_ids).astype(jnp.float32)
    arranged = jnp.dot(
        arrangement,
        combined.reshape(row_count, step_count * columns),
        precision=lax.Precision.HIGHEST,
        preferred_element_type=jnp.float32,
    ).astype(jnp.bfloat16)
    arranged = arranged.reshape(replica_count, share_rows, step_count, columns)
    quarters = lax.all_to_all(arranged, "dp", split_axis=0, concat_axis=0, tiled=True)
    return quarters.transpose(1, 2, 0, 3).reshape(share_rows, step_count, model_width)


def solution(mesh):
    in_specs = (
        P("expert", None, None),
        P("expert", None, None),
        P("expert", None, None),
        P("expert"),
        P("expert"),
        P("expert"),
        P("expert", None, "dp"),
        P("expert", None, "dp"),
        P("expert", "dp", None),
    )
    out_specs = P(("dp", "expert"), None, None)
    return jax.shard_map(body, mesh=mesh, in_specs=in_specs, out_specs=out_specs, check_vma=False)
```

```python
import jax
import jax.numpy as jnp
from jax import lax
from jax.sharding import PartitionSpec as P

MOST_BASE = 16


def exchange_gather(blocks, replica, replica_count):
    pieces = [lax.dynamic_index_in_dim(blocks, replica, 0, keepdims=False)]
    for shift in range(1, replica_count):
        outgoing = lax.dynamic_index_in_dim(
            blocks, (replica + shift) % replica_count, 0, keepdims=False
        )
        pairs = [(i, (i + shift) % replica_count) for i in range(replica_count)]
        pieces.append(lax.ppermute(outgoing, "dp", pairs))
    return jnp.stack(pieces, axis=0)


def exchange_all(block, replica_count):
    pieces = [block]
    for shift in range(1, replica_count):
        pairs = [(i, (i + shift) % replica_count) for i in range(replica_count)]
        pieces.append(lax.ppermute(block, "dp", pairs))
    return jnp.stack(pieces, axis=0)


def body(
    hidden_states, routes, route_weight, finish_step, group_keep, dest_slot, w_gate, w_up, w_down
):
    expert_count = lax.axis_size("expert")
    replica_count = lax.axis_size("dp")
    replica = lax.axis_index("dp")
    row_count, step_count, model_width = hidden_states.shape
    top_count = routes.shape[2]
    hidden_part = w_down.shape[1]
    columns = model_width // replica_count
    tokens = row_count * step_count
    slot_count = min(tokens, max(MOST_BASE, 2 * tokens * top_count // expert_count))
    slot_count = -(-slot_count // replica_count) * replica_count
    part = slot_count // replica_count
    down_blocks = w_down[0].reshape(hidden_part, replica_count, columns).transpose(1, 0, 2)
    down_cols = exchange_gather(down_blocks, replica, replica_count)
    step_ids = lax.broadcasted_iota(jnp.int32, (row_count, step_count), 1)
    live_mask = ((step_ids < finish_step[:, None]) & (group_keep[0] == 1)).reshape(tokens)
    gate_share = route_weight / jnp.sum(route_weight, axis=2, keepdims=True)
    expert_ids = lax.broadcasted_iota(jnp.int32, (1, 1, expert_count), 2)
    picked = (routes.reshape(tokens, top_count, 1) == expert_ids) & live_mask[:, None, None]
    hit_mask = jnp.sum(picked.astype(jnp.int32), axis=1)
    share_wide = jnp.broadcast_to(gate_share.reshape(tokens, top_count, 1), picked.shape)
    weight = jnp.sum(jnp.where(picked, share_wide, jnp.zeros_like(share_wide)), axis=1)
    prior_hits = jnp.cumsum(hit_mask, axis=0) - hit_mask
    flat_inputs = hidden_states.reshape(tokens, model_width)
    chunks = 2 if part % 2 == 0 else 1
    sub = part // chunks
    member_ids = lax.broadcasted_iota(jnp.int32, (1, 1, replica_count, 1), 2)
    within_ids = lax.broadcasted_iota(jnp.int32, (1, 1, 1, sub), 3)
    combined = jnp.zeros((tokens, columns), jnp.float32)
    for chunk in range(chunks):
        slot_ids = replica * part + chunk * sub + lax.broadcasted_iota(jnp.int32, (1, 1, sub), 2)
        placement = (hit_mask[:, :, None] == 1) & (prior_hits[:, :, None] == slot_ids)
        placement = placement.reshape(tokens, expert_count * sub)
        outgoing = lax.dot_general(
            placement.astype(jnp.bfloat16),
            flat_inputs,
            (((0,), (0,)), ((), ())),
            preferred_element_type=jnp.float32,
        ).astype(jnp.bfloat16)
        if chunk == 1:
            down_cols, outgoing = lax.optimization_barrier((down_cols, outgoing))
        arrived = lax.all_to_all(outgoing, "expert", split_axis=0, concat_axis=0, tiled=True)
        gathered = lax.all_gather(arrived, "dp", axis=0, tiled=True)
        gate_part = jnp.dot(gathered, w_gate[0], preferred_element_type=jnp.float32)
        up_part = jnp.dot(gathered, w_up[0], preferred_element_type=jnp.float32)
        activated = (jax.nn.silu(gate_part) * up_part).astype(jnp.bfloat16)
        hidden_all = exchange_all(activated, replica_count)
        expert_cols = lax.dot_general(
            hidden_all,
            down_cols,
            (((0, 2), (0, 1)), ((), ())),
            preferred_element_type=jnp.float32,
        ).astype(jnp.bfloat16)
        by_source = expert_cols.reshape(replica_count, expert_count, sub, columns).transpose(
            1, 0, 2, 3
        )
        returned_rows = lax.all_to_all(by_source, "expert", split_axis=0, concat_axis=0, tiled=True)
        all_slot_ids = member_ids * part + chunk * sub + within_ids
        weighted_place = jnp.where(
            (hit_mask[:, :, None, None] == 1) & (prior_hits[:, :, None, None] == all_slot_ids),
            weight[:, :, None, None],
            0.0,
        ).reshape(tokens, expert_count * replica_count * sub)
        combined = combined + jnp.dot(
            weighted_place,
            returned_rows.reshape(expert_count * replica_count * sub, columns).astype(jnp.float32),
            precision=lax.Precision.HIGHEST,
            preferred_element_type=jnp.float32,
        )
    share_rows = row_count // replica_count
    flat_device = dest_slot // share_rows
    target = flat_device // expert_count * share_rows + dest_slot % share_rows
    position_ids = lax.broadcasted_iota(jnp.int32, (replica_count * share_rows, row_count), 0)
    arrangement = (target[None, :] == position_ids).astype(jnp.float32)
    arranged = jnp.dot(
        arrangement,
        combined.reshape(row_count, step_count * columns),
        precision=lax.Precision.HIGHEST,
        preferred_element_type=jnp.float32,
    ).astype(jnp.bfloat16)
    arranged = arranged.reshape(replica_count, share_rows, step_count, columns)
    quarters = lax.all_to_all(arranged, "dp", split_axis=0, concat_axis=0, tiled=True)
    return quarters.transpose(1, 2, 0, 3).reshape(share_rows, step_count, model_width)


def solution(mesh):
    in_specs = (
        P("expert", None, None),
        P("expert", None, None),
        P("expert", None, None),
        P("expert"),
        P("expert"),
        P("expert"),
        P("expert", None, "dp"),
        P("expert", None, "dp"),
        P("expert", "dp", None),
    )
    out_specs = P(("dp", "expert"), None, None)
    return jax.shard_map(body, mesh=mesh, in_specs=in_specs, out_specs=out_specs, check_vma=False)
```

```python
import jax
import jax.numpy as jnp
from jax import lax
from jax.sharding import PartitionSpec as P

MOST_BASE = 16


def exchange_columns(matrix, replica, replica_count):
    width = matrix.shape[1] // replica_count
    pieces = [lax.dynamic_slice_in_dim(matrix, replica * width, width, axis=1)]
    for shift in range(1, replica_count):
        start = ((replica + shift) % replica_count) * width
        outgoing = lax.dynamic_slice_in_dim(matrix, start, width, axis=1)
        pairs = [(i, (i + shift) % replica_count) for i in range(replica_count)]
        pieces.append(lax.ppermute(outgoing, "dp", pairs))
    return pieces


def exchange_all(block, replica_count):
    pieces = [block]
    for shift in range(1, replica_count):
        pairs = [(i, (i + shift) % replica_count) for i in range(replica_count)]
        pieces.append(lax.ppermute(block, "dp", pairs))
    return pieces


def body(
    hidden_states, routes, route_weight, finish_step, group_keep, dest_slot, w_gate, w_up, w_down
):
    expert_count = lax.axis_size("expert")
    replica_count = lax.axis_size("dp")
    replica = lax.axis_index("dp")
    row_count, step_count, model_width = hidden_states.shape
    top_count = routes.shape[2]
    hidden_part = w_down.shape[1]
    columns = model_width // replica_count
    tokens = row_count * step_count
    slot_count = min(tokens, max(MOST_BASE, 2 * tokens * top_count // expert_count))
    slot_count = -(-slot_count // replica_count) * replica_count
    part = slot_count // replica_count
    down_cols = exchange_columns(w_down[0], replica, replica_count)
    step_ids = lax.broadcasted_iota(jnp.int32, (row_count, step_count), 1)
    live_mask = ((step_ids < finish_step[:, None]) & (group_keep[0] == 1)).reshape(tokens)
    gate_share = route_weight / jnp.sum(route_weight, axis=2, keepdims=True)
    expert_ids = lax.broadcasted_iota(jnp.int32, (1, 1, expert_count), 2)
    picked = (routes.reshape(tokens, top_count, 1) == expert_ids) & live_mask[:, None, None]
    hit_mask = jnp.sum(picked.astype(jnp.int32), axis=1)
    share_wide = jnp.broadcast_to(gate_share.reshape(tokens, top_count, 1), picked.shape)
    weight = jnp.sum(jnp.where(picked, share_wide, jnp.zeros_like(share_wide)), axis=1)
    prior_hits = jnp.cumsum(hit_mask, axis=0) - hit_mask
    flat_inputs = hidden_states.reshape(tokens, model_width)
    chunks = 2 if part % 2 == 0 else 1
    sub = part // chunks
    member_ids = lax.broadcasted_iota(jnp.int32, (1, 1, replica_count, 1), 2)
    within_ids = lax.broadcasted_iota(jnp.int32, (1, 1, 1, sub), 3)
    combined = jnp.zeros((tokens, columns), jnp.float32)
    for chunk in range(chunks):
        slot_ids = replica * part + chunk * sub + lax.broadcasted_iota(jnp.int32, (1, 1, sub), 2)
        placement = (hit_mask[:, :, None] == 1) & (prior_hits[:, :, None] == slot_ids)
        placement = placement.reshape(tokens, expert_count * sub)
        outgoing = lax.dot_general(
            placement.astype(jnp.bfloat16),
            flat_inputs,
            (((0,), (0,)), ((), ())),
            preferred_element_type=jnp.float32,
        ).astype(jnp.bfloat16)
        arrived = lax.all_to_all(outgoing, "expert", split_axis=0, concat_axis=0, tiled=True)
        if chunk == 0:
            down_cols, arrived = lax.optimization_barrier((down_cols, arrived))
        gathered = lax.all_gather(arrived, "dp", axis=0, tiled=True)
        gate_part = jnp.dot(gathered, w_gate[0], preferred_element_type=jnp.float32)
        up_part = jnp.dot(gathered, w_up[0], preferred_element_type=jnp.float32)
        activated = (jax.nn.silu(gate_part) * up_part).astype(jnp.bfloat16)
        hidden_all = exchange_all(activated, replica_count)
        expert_cols = jnp.dot(hidden_all[0], down_cols[0], preferred_element_type=jnp.float32)
        for shift in range(1, replica_count):
            expert_cols = expert_cols + jnp.dot(
                hidden_all[shift], down_cols[shift], preferred_element_type=jnp.float32
            )
        expert_cols = expert_cols.astype(jnp.bfloat16)
        by_source = expert_cols.reshape(replica_count, expert_count, sub, columns).transpose(
            1, 0, 2, 3
        )
        returned_rows = lax.all_to_all(by_source, "expert", split_axis=0, concat_axis=0, tiled=True)
        all_slot_ids = member_ids * part + chunk * sub + within_ids
        weighted_place = jnp.where(
            (hit_mask[:, :, None, None] == 1) & (prior_hits[:, :, None, None] == all_slot_ids),
            weight[:, :, None, None],
            0.0,
        ).reshape(tokens, expert_count * replica_count * sub)
        combined = combined + jnp.dot(
            weighted_place,
            returned_rows.reshape(expert_count * replica_count * sub, columns).astype(jnp.float32),
            precision=lax.Precision.HIGHEST,
            preferred_element_type=jnp.float32,
        )
    share_rows = row_count // replica_count
    flat_device = dest_slot // share_rows
    target = flat_device // expert_count * share_rows + dest_slot % share_rows
    position_ids = lax.broadcasted_iota(jnp.int32, (replica_count * share_rows, row_count), 0)
    arrangement = (target[None, :] == position_ids).astype(jnp.float32)
    arranged = jnp.dot(
        arrangement,
        combined.reshape(row_count, step_count * columns),
        precision=lax.Precision.HIGHEST,
        preferred_element_type=jnp.float32,
    ).astype(jnp.bfloat16)
    arranged = arranged.reshape(replica_count, share_rows, step_count, columns)
    quarters = lax.all_to_all(arranged, "dp", split_axis=0, concat_axis=0, tiled=True)
    return quarters.transpose(1, 2, 0, 3).reshape(share_rows, step_count, model_width)


def solution(mesh):
    in_specs = (
        P("expert", None, None),
        P("expert", None, None),
        P("expert", None, None),
        P("expert"),
        P("expert"),
        P("expert"),
        P("expert", None, "dp"),
        P("expert", None, "dp"),
        P("expert", "dp", None),
    )
    out_specs = P(("dp", "expert"), None, None)
    return jax.shard_map(body, mesh=mesh, in_specs=in_specs, out_specs=out_specs, check_vma=False)
```

```python
import jax
import jax.numpy as jnp
from jax import lax
from jax.sharding import PartitionSpec as P

MOST_BASE = 16


def exchange_columns(matrix, replica, replica_count):
    width = matrix.shape[1] // replica_count
    pieces = [lax.dynamic_slice_in_dim(matrix, replica * width, width, axis=1)]
    for shift in range(1, replica_count):
        start = ((replica + shift) % replica_count) * width
        outgoing = lax.dynamic_slice_in_dim(matrix, start, width, axis=1)
        pairs = [(i, (i + shift) % replica_count) for i in range(replica_count)]
        pieces.append(lax.ppermute(outgoing, "dp", pairs))
    return pieces


def exchange_all(block, replica_count):
    pieces = [block]
    for shift in range(1, replica_count):
        pairs = [(i, (i + shift) % replica_count) for i in range(replica_count)]
        pieces.append(lax.ppermute(block, "dp", pairs))
    return pieces


def body(
    hidden_states, routes, route_weight, finish_step, group_keep, dest_slot, w_gate, w_up, w_down
):
    expert_count = lax.axis_size("expert")
    replica_count = lax.axis_size("dp")
    replica = lax.axis_index("dp")
    row_count, step_count, model_width = hidden_states.shape
    top_count = routes.shape[2]
    hidden_part = w_down.shape[1]
    columns = model_width // replica_count
    tokens = row_count * step_count
    slot_count = min(tokens, max(MOST_BASE, 2 * tokens * top_count // expert_count))
    slot_count = -(-slot_count // replica_count) * replica_count
    part = slot_count // replica_count
    down_cols = exchange_columns(w_down[0], replica, replica_count)
    step_ids = lax.broadcasted_iota(jnp.int32, (row_count, step_count), 1)
    live_mask = ((step_ids < finish_step[:, None]) & (group_keep[0] == 1)).reshape(tokens)
    gate_share = route_weight / jnp.sum(route_weight, axis=2, keepdims=True)
    expert_ids = lax.broadcasted_iota(jnp.int32, (1, 1, expert_count), 2)
    picked = (routes.reshape(tokens, top_count, 1) == expert_ids) & live_mask[:, None, None]
    hit_mask = jnp.sum(picked.astype(jnp.int32), axis=1)
    share_wide = jnp.broadcast_to(gate_share.reshape(tokens, top_count, 1), picked.shape)
    weight = jnp.sum(jnp.where(picked, share_wide, jnp.zeros_like(share_wide)), axis=1)
    prior_hits = jnp.cumsum(hit_mask, axis=0) - hit_mask
    flat_inputs = hidden_states.reshape(tokens, model_width)
    chunks = 2 if part % 2 == 0 else 1
    sub = part // chunks
    member_ids = lax.broadcasted_iota(jnp.int32, (1, 1, replica_count, 1), 2)
    within_ids = lax.broadcasted_iota(jnp.int32, (1, 1, 1, sub), 3)
    combined = jnp.zeros((tokens, columns), jnp.float32)
    for chunk in range(chunks):
        slot_ids = replica * part + chunk * sub + lax.broadcasted_iota(jnp.int32, (1, 1, sub), 2)
        placement = (hit_mask[:, :, None] == 1) & (prior_hits[:, :, None] == slot_ids)
        placement = placement.reshape(tokens, expert_count * sub)
        outgoing = lax.dot_general(
            placement.astype(jnp.bfloat16),
            flat_inputs,
            (((0,), (0,)), ((), ())),
            preferred_element_type=jnp.float32,
        ).astype(jnp.bfloat16)
        if chunk == 1:
            down_cols, outgoing = lax.optimization_barrier((down_cols, outgoing))
        arrived = lax.all_to_all(outgoing, "expert", split_axis=0, concat_axis=0, tiled=True)
        gathered = lax.all_gather(arrived, "dp", axis=0, tiled=True)
        gate_part = jnp.dot(gathered, w_gate[0], preferred_element_type=jnp.float32)
        up_part = jnp.dot(gathered, w_up[0], preferred_element_type=jnp.float32)
        activated = (jax.nn.silu(gate_part) * up_part).astype(jnp.bfloat16)
        hidden_all = exchange_all(activated, replica_count)
        expert_cols = jnp.dot(hidden_all[0], down_cols[0], preferred_element_type=jnp.float32)
        for shift in range(1, replica_count):
            expert_cols = expert_cols + jnp.dot(
                hidden_all[shift], down_cols[shift], preferred_element_type=jnp.float32
            )
        expert_cols = expert_cols.astype(jnp.bfloat16)
        by_source = expert_cols.reshape(replica_count, expert_count, sub, columns).transpose(
            1, 0, 2, 3
        )
        returned_rows = lax.all_to_all(by_source, "expert", split_axis=0, concat_axis=0, tiled=True)
        all_slot_ids = member_ids * part + chunk * sub + within_ids
        weighted_place = jnp.where(
            (hit_mask[:, :, None, None] == 1) & (prior_hits[:, :, None, None] == all_slot_ids),
            weight[:, :, None, None],
            0.0,
        ).reshape(tokens, expert_count * replica_count * sub)
        combined = combined + jnp.dot(
            weighted_place,
            returned_rows.reshape(expert_count * replica_count * sub, columns).astype(jnp.float32),
            precision=lax.Precision.HIGHEST,
            preferred_element_type=jnp.float32,
        )
    share_rows = row_count // replica_count
    flat_device = dest_slot // share_rows
    target = flat_device // expert_count * share_rows + dest_slot % share_rows
    position_ids = lax.broadcasted_iota(jnp.int32, (replica_count * share_rows, row_count), 0)
    arrangement = (target[None, :] == position_ids).astype(jnp.float32)
    arranged = jnp.dot(
        arrangement,
        combined.reshape(row_count, step_count * columns),
        precision=lax.Precision.HIGHEST,
        preferred_element_type=jnp.float32,
    ).astype(jnp.bfloat16)
    arranged = arranged.reshape(replica_count, share_rows, step_count, columns)
    quarters = lax.all_to_all(arranged, "dp", split_axis=0, concat_axis=0, tiled=True)
    return quarters.transpose(1, 2, 0, 3).reshape(share_rows, step_count, model_width)


def solution(mesh):
    in_specs = (
        P("expert", None, None),
        P("expert", None, None),
        P("expert", None, None),
        P("expert"),
        P("expert"),
        P("expert"),
        P("expert", None, "dp"),
        P("expert", None, "dp"),
        P("expert", "dp", None),
    )
    out_specs = P(("dp", "expert"), None, None)
    return jax.shard_map(body, mesh=mesh, in_specs=in_specs, out_specs=out_specs, check_vma=False)
```

```python
import jax
import jax.numpy as jnp
from jax import lax
from jax.sharding import PartitionSpec as P

MOST_BASE = 16


def exchange_columns(matrix, replica, replica_count):
    width = matrix.shape[1] // replica_count
    pieces = [lax.dynamic_slice_in_dim(matrix, replica * width, width, axis=1)]
    for shift in range(1, replica_count):
        start = ((replica + shift) % replica_count) * width
        outgoing = lax.dynamic_slice_in_dim(matrix, start, width, axis=1)
        pairs = [(i, (i + shift) % replica_count) for i in range(replica_count)]
        pieces.append(lax.ppermute(outgoing, "dp", pairs))
    return pieces


def exchange_all(block, replica_count):
    pieces = [block]
    for shift in range(1, replica_count):
        pairs = [(i, (i + shift) % replica_count) for i in range(replica_count)]
        pieces.append(lax.ppermute(block, "dp", pairs))
    return pieces


def body(
    hidden_states, routes, route_weight, finish_step, group_keep, dest_slot, w_gate, w_up, w_down
):
    expert_count = lax.axis_size("expert")
    replica_count = lax.axis_size("dp")
    replica = lax.axis_index("dp")
    row_count, step_count, model_width = hidden_states.shape
    top_count = routes.shape[2]
    hidden_part = w_down.shape[1]
    columns = model_width // replica_count
    tokens = row_count * step_count
    slot_count = min(tokens, max(MOST_BASE, 2 * tokens * top_count // expert_count))
    slot_count = -(-slot_count // replica_count) * replica_count
    part = slot_count // replica_count
    down_cols = exchange_columns(w_down[0], replica, replica_count)
    step_ids = lax.broadcasted_iota(jnp.int32, (row_count, step_count), 1)
    live_mask = ((step_ids < finish_step[:, None]) & (group_keep[0] == 1)).reshape(tokens)
    gate_share = route_weight / jnp.sum(route_weight, axis=2, keepdims=True)
    expert_ids = lax.broadcasted_iota(jnp.int32, (1, 1, expert_count), 2)
    picked = (routes.reshape(tokens, top_count, 1) == expert_ids) & live_mask[:, None, None]
    hit_mask = jnp.sum(picked.astype(jnp.int32), axis=1)
    share_wide = jnp.broadcast_to(gate_share.reshape(tokens, top_count, 1), picked.shape)
    weight = jnp.sum(jnp.where(picked, share_wide, jnp.zeros_like(share_wide)), axis=1)
    prior_hits = jnp.cumsum(hit_mask, axis=0) - hit_mask
    flat_inputs = hidden_states.reshape(tokens, model_width)
    chunks = 2 if part % 2 == 0 else 1
    sub = part // chunks
    member_ids = lax.broadcasted_iota(jnp.int32, (1, 1, replica_count, 1), 2)
    within_ids = lax.broadcasted_iota(jnp.int32, (1, 1, 1, sub), 3)
    combined = jnp.zeros((tokens, columns), jnp.float32)
    for chunk in range(chunks):
        slot_ids = replica * part + chunk * sub + lax.broadcasted_iota(jnp.int32, (1, 1, sub), 2)
        placement = (hit_mask[:, :, None] == 1) & (prior_hits[:, :, None] == slot_ids)
        placement = placement.reshape(tokens, expert_count * sub)
        outgoing = lax.dot_general(
            placement.astype(jnp.bfloat16),
            flat_inputs,
            (((0,), (0,)), ((), ())),
            preferred_element_type=jnp.float32,
        ).astype(jnp.bfloat16)
        if chunk == 1:
            down_cols, outgoing = lax.optimization_barrier((down_cols, outgoing))
        arrived = lax.all_to_all(outgoing, "expert", split_axis=0, concat_axis=0, tiled=True)
        gathered = lax.all_gather(arrived, "dp", axis=0, tiled=True)
        gate_part = jnp.dot(gathered, w_gate[0], preferred_element_type=jnp.float32)
        up_part = jnp.dot(gathered, w_up[0], preferred_element_type=jnp.float32)
        activated = (jax.nn.silu(gate_part) * up_part).astype(jnp.bfloat16)
        gathered_hidden = lax.all_gather(activated, "dp", axis=0, tiled=False)
        hidden_all = [
            lax.dynamic_index_in_dim(
                gathered_hidden, (replica - shift) % replica_count, 0, keepdims=False
            )
            for shift in range(replica_count)
        ]
        expert_cols = jnp.dot(hidden_all[0], down_cols[0], preferred_element_type=jnp.float32)
        for shift in range(1, replica_count):
            expert_cols = expert_cols + jnp.dot(
                hidden_all[shift], down_cols[shift], preferred_element_type=jnp.float32
            )
        expert_cols = expert_cols.astype(jnp.bfloat16)
        by_source = expert_cols.reshape(replica_count, expert_count, sub, columns).transpose(
            1, 0, 2, 3
        )
        returned_rows = lax.all_to_all(by_source, "expert", split_axis=0, concat_axis=0, tiled=True)
        all_slot_ids = member_ids * part + chunk * sub + within_ids
        weighted_place = jnp.where(
            (hit_mask[:, :, None, None] == 1) & (prior_hits[:, :, None, None] == all_slot_ids),
            weight[:, :, None, None],
            0.0,
        ).reshape(tokens, expert_count * replica_count * sub)
        combined = combined + jnp.dot(
            weighted_place,
            returned_rows.reshape(expert_count * replica_count * sub, columns).astype(jnp.float32),
            precision=lax.Precision.HIGHEST,
            preferred_element_type=jnp.float32,
        )
    share_rows = row_count // replica_count
    flat_device = dest_slot // share_rows
    target = flat_device // expert_count * share_rows + dest_slot % share_rows
    position_ids = lax.broadcasted_iota(jnp.int32, (replica_count * share_rows, row_count), 0)
    arrangement = (target[None, :] == position_ids).astype(jnp.float32)
    arranged = jnp.dot(
        arrangement,
        combined.reshape(row_count, step_count * columns),
        precision=lax.Precision.HIGHEST,
        preferred_element_type=jnp.float32,
    ).astype(jnp.bfloat16)
    arranged = arranged.reshape(replica_count, share_rows, step_count, columns)
    quarters = lax.all_to_all(arranged, "dp", split_axis=0, concat_axis=0, tiled=True)
    return quarters.transpose(1, 2, 0, 3).reshape(share_rows, step_count, model_width)


def solution(mesh):
    in_specs = (
        P("expert", None, None),
        P("expert", None, None),
        P("expert", None, None),
        P("expert"),
        P("expert"),
        P("expert"),
        P("expert", None, "dp"),
        P("expert", None, "dp"),
        P("expert", "dp", None),
    )
    out_specs = P(("dp", "expert"), None, None)
    return jax.shard_map(body, mesh=mesh, in_specs=in_specs, out_specs=out_specs, check_vma=False)
```

```python
import jax
import jax.numpy as jnp
from jax import lax
from jax.sharding import PartitionSpec as P

MOST_BASE = 16


def exchange_columns(matrix, replica, replica_count):
    width = matrix.shape[1] // replica_count
    pieces = [lax.dynamic_slice_in_dim(matrix, replica * width, width, axis=1)]
    for shift in range(1, replica_count):
        start = ((replica + shift) % replica_count) * width
        outgoing = lax.dynamic_slice_in_dim(matrix, start, width, axis=1)
        pairs = [(i, (i + shift) % replica_count) for i in range(replica_count)]
        pieces.append(lax.ppermute(outgoing, "dp", pairs))
    return pieces


def exchange_all(block, replica_count):
    pieces = [block]
    for shift in range(1, replica_count):
        pairs = [(i, (i + shift) % replica_count) for i in range(replica_count)]
        pieces.append(lax.ppermute(block, "dp", pairs))
    return pieces


def body(
    hidden_states, routes, route_weight, finish_step, group_keep, dest_slot, w_gate, w_up, w_down
):
    expert_count = lax.axis_size("expert")
    replica_count = lax.axis_size("dp")
    replica = lax.axis_index("dp")
    row_count, step_count, model_width = hidden_states.shape
    top_count = routes.shape[2]
    hidden_part = w_down.shape[1]
    columns = model_width // replica_count
    tokens = row_count * step_count
    slot_count = min(tokens, max(MOST_BASE, 2 * tokens * top_count // expert_count))
    slot_count = -(-slot_count // replica_count) * replica_count
    part = slot_count // replica_count
    down_cols = exchange_columns(w_down[0], replica, replica_count)
    step_ids = lax.broadcasted_iota(jnp.int32, (row_count, step_count), 1)
    live_mask = ((step_ids < finish_step[:, None]) & (group_keep[0] == 1)).reshape(tokens)
    gate_share = route_weight / jnp.sum(route_weight, axis=2, keepdims=True)
    expert_ids = lax.broadcasted_iota(jnp.int32, (1, 1, expert_count), 2)
    picked = (routes.reshape(tokens, top_count, 1) == expert_ids) & live_mask[:, None, None]
    hit_mask = jnp.sum(picked.astype(jnp.int32), axis=1)
    share_wide = jnp.broadcast_to(gate_share.reshape(tokens, top_count, 1), picked.shape)
    weight = jnp.sum(jnp.where(picked, share_wide, jnp.zeros_like(share_wide)), axis=1)
    prior_hits = jnp.cumsum(hit_mask, axis=0) - hit_mask
    flat_inputs = hidden_states.reshape(tokens, model_width)
    chunks = 2 if part % 2 == 0 else 1
    sub = part // chunks
    member_ids = lax.broadcasted_iota(jnp.int32, (1, 1, replica_count, 1), 2)
    within_ids = lax.broadcasted_iota(jnp.int32, (1, 1, 1, sub), 3)
    combined = jnp.zeros((tokens, columns), jnp.float32)
    outgoings = []
    for chunk in range(chunks):
        slot_ids = replica * part + chunk * sub + lax.broadcasted_iota(jnp.int32, (1, 1, sub), 2)
        placement = (hit_mask[:, :, None] == 1) & (prior_hits[:, :, None] == slot_ids)
        placement = placement.reshape(tokens, expert_count * sub)
        outgoings.append(
            lax.dot_general(
                placement.astype(jnp.bfloat16),
                flat_inputs,
                (((0,), (0,)), ((), ())),
                preferred_element_type=jnp.float32,
            ).astype(jnp.bfloat16)
        )
    arrivals = [lax.all_to_all(outgoings[0], "expert", split_axis=0, concat_axis=0, tiled=True)]
    fenced = lax.optimization_barrier((down_cols, arrivals[0], outgoings[1:]))
    down_cols, arrivals[0], rest = fenced
    for outgoing in rest:
        arrivals.append(lax.all_to_all(outgoing, "expert", split_axis=0, concat_axis=0, tiled=True))
    for chunk in range(chunks):
        arrived = arrivals[chunk]
        gathered = lax.all_gather(arrived, "dp", axis=0, tiled=True)
        gate_part = jnp.dot(gathered, w_gate[0], preferred_element_type=jnp.float32)
        up_part = jnp.dot(gathered, w_up[0], preferred_element_type=jnp.float32)
        activated = (jax.nn.silu(gate_part) * up_part).astype(jnp.bfloat16)
        gathered_hidden = lax.all_gather(activated, "dp", axis=0, tiled=False)
        hidden_all = [
            lax.dynamic_index_in_dim(
                gathered_hidden, (replica - shift) % replica_count, 0, keepdims=False
            )
            for shift in range(replica_count)
        ]
        expert_cols = jnp.dot(hidden_all[0], down_cols[0], preferred_element_type=jnp.float32)
        for shift in range(1, replica_count):
            expert_cols = expert_cols + jnp.dot(
                hidden_all[shift], down_cols[shift], preferred_element_type=jnp.float32
            )
        expert_cols = expert_cols.astype(jnp.bfloat16)
        by_source = expert_cols.reshape(replica_count, expert_count, sub, columns).transpose(
            1, 0, 2, 3
        )
        returned_rows = lax.all_to_all(by_source, "expert", split_axis=0, concat_axis=0, tiled=True)
        all_slot_ids = member_ids * part + chunk * sub + within_ids
        weighted_place = jnp.where(
            (hit_mask[:, :, None, None] == 1) & (prior_hits[:, :, None, None] == all_slot_ids),
            weight[:, :, None, None],
            0.0,
        ).reshape(tokens, expert_count * replica_count * sub)
        combined = combined + jnp.dot(
            weighted_place,
            returned_rows.reshape(expert_count * replica_count * sub, columns).astype(jnp.float32),
            precision=lax.Precision.HIGHEST,
            preferred_element_type=jnp.float32,
        )
    share_rows = row_count // replica_count
    flat_device = dest_slot // share_rows
    target = flat_device // expert_count * share_rows + dest_slot % share_rows
    position_ids = lax.broadcasted_iota(jnp.int32, (replica_count * share_rows, row_count), 0)
    arrangement = (target[None, :] == position_ids).astype(jnp.float32)
    arranged = jnp.dot(
        arrangement,
        combined.reshape(row_count, step_count * columns),
        precision=lax.Precision.HIGHEST,
        preferred_element_type=jnp.float32,
    ).astype(jnp.bfloat16)
    arranged = arranged.reshape(replica_count, share_rows, step_count, columns)
    quarters = lax.all_to_all(arranged, "dp", split_axis=0, concat_axis=0, tiled=True)
    return quarters.transpose(1, 2, 0, 3).reshape(share_rows, step_count, model_width)


def solution(mesh):
    in_specs = (
        P("expert", None, None),
        P("expert", None, None),
        P("expert", None, None),
        P("expert"),
        P("expert"),
        P("expert"),
        P("expert", None, "dp"),
        P("expert", None, "dp"),
        P("expert", "dp", None),
    )
    out_specs = P(("dp", "expert"), None, None)
    return jax.shard_map(body, mesh=mesh, in_specs=in_specs, out_specs=out_specs, check_vma=False)
```

```python
import jax
import jax.numpy as jnp
from jax import lax
from jax.sharding import PartitionSpec as P

MOST_BASE = 16


def exchange_gather(matrix, replica, replica_count):
    width = matrix.shape[1] // replica_count
    pieces = [lax.dynamic_slice_in_dim(matrix, replica * width, width, axis=1)]
    for shift in range(1, replica_count):
        start = ((replica + shift) % replica_count) * width
        outgoing = lax.dynamic_slice_in_dim(matrix, start, width, axis=1)
        pairs = [(i, (i + shift) % replica_count) for i in range(replica_count)]
        pieces.append(lax.ppermute(outgoing, "dp", pairs))
    return jnp.stack(pieces, axis=0)


def exchange_all(block, replica_count):
    pieces = [block]
    for shift in range(1, replica_count):
        pairs = [(i, (i + shift) % replica_count) for i in range(replica_count)]
        pieces.append(lax.ppermute(block, "dp", pairs))
    return jnp.stack(pieces, axis=0)


def body(
    hidden_states, routes, route_weight, finish_step, group_keep, dest_slot, w_gate, w_up, w_down
):
    expert_count = lax.axis_size("expert")
    replica_count = lax.axis_size("dp")
    replica = lax.axis_index("dp")
    row_count, step_count, model_width = hidden_states.shape
    top_count = routes.shape[2]
    hidden_part = w_down.shape[1]
    columns = model_width // replica_count
    tokens = row_count * step_count
    slot_count = min(tokens, max(MOST_BASE, 2 * tokens * top_count // expert_count))
    slot_count = -(-slot_count // replica_count) * replica_count
    part = slot_count // replica_count
    down_cols = exchange_gather(w_down[0], replica, replica_count)
    step_ids = lax.broadcasted_iota(jnp.int32, (row_count, step_count), 1)
    live_mask = ((step_ids < finish_step[:, None]) & (group_keep[0] == 1)).reshape(tokens)
    gate_share = route_weight / jnp.sum(route_weight, axis=2, keepdims=True)
    expert_ids = lax.broadcasted_iota(jnp.int32, (1, 1, expert_count), 2)
    picked = (routes.reshape(tokens, top_count, 1) == expert_ids) & live_mask[:, None, None]
    hit_mask = jnp.sum(picked.astype(jnp.int32), axis=1)
    share_wide = jnp.broadcast_to(gate_share.reshape(tokens, top_count, 1), picked.shape)
    weight = jnp.sum(jnp.where(picked, share_wide, jnp.zeros_like(share_wide)), axis=1)
    prior_hits = jnp.cumsum(hit_mask, axis=0) - hit_mask
    flat_inputs = hidden_states.reshape(tokens, model_width)
    chunks = 2 if part % 2 == 0 else 1
    sub = part // chunks
    member_ids = lax.broadcasted_iota(jnp.int32, (1, 1, replica_count, 1), 2)
    within_ids = lax.broadcasted_iota(jnp.int32, (1, 1, 1, sub), 3)
    combined = jnp.zeros((tokens, columns), jnp.float32)
    for chunk in range(chunks):
        slot_ids = replica * part + chunk * sub + lax.broadcasted_iota(jnp.int32, (1, 1, sub), 2)
        placement = (hit_mask[:, :, None] == 1) & (prior_hits[:, :, None] == slot_ids)
        placement = placement.reshape(tokens, expert_count * sub)
        outgoing = lax.dot_general(
            placement.astype(jnp.bfloat16),
            flat_inputs,
            (((0,), (0,)), ((), ())),
            preferred_element_type=jnp.float32,
        ).astype(jnp.bfloat16)
        if chunk == 1:
            down_cols, outgoing = lax.optimization_barrier((down_cols, outgoing))
        arrived = lax.all_to_all(outgoing, "expert", split_axis=0, concat_axis=0, tiled=True)
        gathered = lax.all_gather(arrived, "dp", axis=0, tiled=True)
        gate_part = jnp.dot(gathered, w_gate[0], preferred_element_type=jnp.float32)
        up_part = jnp.dot(gathered, w_up[0], preferred_element_type=jnp.float32)
        activated = (jax.nn.silu(gate_part) * up_part).astype(jnp.bfloat16)
        hidden_all = exchange_all(activated, replica_count)
        expert_cols = lax.dot_general(
            hidden_all,
            down_cols,
            (((0, 2), (0, 1)), ((), ())),
            preferred_element_type=jnp.float32,
        ).astype(jnp.bfloat16)
        by_source = expert_cols.reshape(replica_count, expert_count, sub, columns).transpose(
            1, 0, 2, 3
        )
        returned_rows = lax.all_to_all(by_source, "expert", split_axis=0, concat_axis=0, tiled=True)
        all_slot_ids = member_ids * part + chunk * sub + within_ids
        weighted_place = jnp.where(
            (hit_mask[:, :, None, None] == 1) & (prior_hits[:, :, None, None] == all_slot_ids),
            weight[:, :, None, None],
            0.0,
        ).reshape(tokens, expert_count * replica_count * sub)
        combined = combined + jnp.dot(
            weighted_place,
            returned_rows.reshape(expert_count * replica_count * sub, columns).astype(jnp.float32),
            precision=lax.Precision.HIGHEST,
            preferred_element_type=jnp.float32,
        )
    share_rows = row_count // replica_count
    flat_device = dest_slot // share_rows
    target = flat_device // expert_count * share_rows + dest_slot % share_rows
    position_ids = lax.broadcasted_iota(jnp.int32, (replica_count * share_rows, row_count), 0)
    arrangement = (target[None, :] == position_ids).astype(jnp.float32)
    arranged = jnp.dot(
        arrangement,
        combined.reshape(row_count, step_count * columns),
        precision=lax.Precision.HIGHEST,
        preferred_element_type=jnp.float32,
    ).astype(jnp.bfloat16)
    arranged = arranged.reshape(replica_count, share_rows, step_count, columns)
    quarters = lax.all_to_all(arranged, "dp", split_axis=0, concat_axis=0, tiled=True)
    return quarters.transpose(1, 2, 0, 3).reshape(share_rows, step_count, model_width)


def solution(mesh):
    in_specs = (
        P("expert", None, None),
        P("expert", None, None),
        P("expert", None, None),
        P("expert"),
        P("expert"),
        P("expert"),
        P("expert", None, "dp"),
        P("expert", None, "dp"),
        P("expert", "dp", None),
    )
    out_specs = P(("dp", "expert"), None, None)
    return jax.shard_map(body, mesh=mesh, in_specs=in_specs, out_specs=out_specs, check_vma=False)
```

```python
import jax
import jax.numpy as jnp
from jax import lax
from jax.sharding import PartitionSpec as P

MOST_BASE = 16


def exchange_gather(matrix, replica, replica_count):
    width = matrix.shape[1] // replica_count
    pieces = [lax.dynamic_slice_in_dim(matrix, replica * width, width, axis=1)]
    for shift in range(1, replica_count):
        start = ((replica + shift) % replica_count) * width
        outgoing = lax.dynamic_slice_in_dim(matrix, start, width, axis=1)
        pairs = [(i, (i + shift) % replica_count) for i in range(replica_count)]
        pieces.append(lax.ppermute(outgoing, "dp", pairs))
    return jnp.stack(pieces, axis=0)


def exchange_all(block, replica_count):
    pieces = [block]
    for shift in range(1, replica_count):
        pairs = [(i, (i + shift) % replica_count) for i in range(replica_count)]
        pieces.append(lax.ppermute(block, "dp", pairs))
    return jnp.stack(pieces, axis=0)


def body(
    hidden_states, routes, route_weight, finish_step, group_keep, dest_slot, w_gate, w_up, w_down
):
    expert_count = lax.axis_size("expert")
    replica_count = lax.axis_size("dp")
    replica = lax.axis_index("dp")
    row_count, step_count, model_width = hidden_states.shape
    top_count = routes.shape[2]
    hidden_part = w_down.shape[1]
    columns = model_width // replica_count
    tokens = row_count * step_count
    slot_count = min(tokens, max(MOST_BASE, 2 * tokens * top_count // expert_count))
    slot_count = -(-slot_count // replica_count) * replica_count
    part = slot_count // replica_count
    down_cols = exchange_gather(w_down[0], replica, replica_count)
    step_ids = lax.broadcasted_iota(jnp.int32, (row_count, step_count), 1)
    live_mask = ((step_ids < finish_step[:, None]) & (group_keep[0] == 1)).reshape(tokens)
    gate_share = route_weight / jnp.sum(route_weight, axis=2, keepdims=True)
    expert_ids = lax.broadcasted_iota(jnp.int32, (1, 1, expert_count), 2)
    picked = (routes.reshape(tokens, top_count, 1) == expert_ids) & live_mask[:, None, None]
    hit_mask = jnp.sum(picked.astype(jnp.int32), axis=1)
    share_wide = jnp.broadcast_to(gate_share.reshape(tokens, top_count, 1), picked.shape)
    weight = jnp.sum(jnp.where(picked, share_wide, jnp.zeros_like(share_wide)), axis=1)
    prior_hits = jnp.cumsum(hit_mask, axis=0) - hit_mask
    flat_inputs = hidden_states.reshape(tokens, model_width)
    chunks = 2 if part % 2 == 0 else 1
    sub = part // chunks
    member_ids = lax.broadcasted_iota(jnp.int32, (1, 1, replica_count, 1), 2)
    within_ids = lax.broadcasted_iota(jnp.int32, (1, 1, 1, sub), 3)
    share_rows = row_count // replica_count
    flat_device = dest_slot // share_rows
    target = flat_device // expert_count * share_rows + dest_slot % share_rows
    position_ids = lax.broadcasted_iota(jnp.int32, (replica_count * share_rows, row_count), 0)
    arrangement = (target[None, :] == position_ids).astype(jnp.float32)
    weight = jnp.dot(
        arrangement,
        weight.reshape(row_count, step_count * expert_count),
        precision=lax.Precision.HIGHEST,
        preferred_element_type=jnp.float32,
    ).reshape(tokens, expert_count)
    hit_arranged = jnp.dot(
        arrangement,
        hit_mask.reshape(row_count, step_count * expert_count).astype(jnp.float32),
        precision=lax.Precision.HIGHEST,
    ).reshape(tokens, expert_count)
    prior_arranged = jnp.dot(
        arrangement,
        prior_hits.reshape(row_count, step_count * expert_count).astype(jnp.float32),
        precision=lax.Precision.HIGHEST,
    ).reshape(tokens, expert_count)
    combined = jnp.zeros((tokens, columns), jnp.float32)
    for chunk in range(chunks):
        slot_ids = replica * part + chunk * sub + lax.broadcasted_iota(jnp.int32, (1, 1, sub), 2)
        placement = (hit_mask[:, :, None] == 1) & (prior_hits[:, :, None] == slot_ids)
        placement = placement.reshape(tokens, expert_count * sub)
        outgoing = lax.dot_general(
            placement.astype(jnp.bfloat16),
            flat_inputs,
            (((0,), (0,)), ((), ())),
            preferred_element_type=jnp.float32,
        ).astype(jnp.bfloat16)
        if chunk == 1:
            down_cols, outgoing = lax.optimization_barrier((down_cols, outgoing))
        arrived = lax.all_to_all(outgoing, "expert", split_axis=0, concat_axis=0, tiled=True)
        gathered = lax.all_gather(arrived, "dp", axis=0, tiled=True)
        gate_part = jnp.dot(gathered, w_gate[0], preferred_element_type=jnp.float32)
        up_part = jnp.dot(gathered, w_up[0], preferred_element_type=jnp.float32)
        activated = (jax.nn.silu(gate_part) * up_part).astype(jnp.bfloat16)
        hidden_all = exchange_all(activated, replica_count)
        expert_cols = lax.dot_general(
            hidden_all,
            down_cols,
            (((0, 2), (0, 1)), ((), ())),
            preferred_element_type=jnp.float32,
        ).astype(jnp.bfloat16)
        by_source = expert_cols.reshape(replica_count, expert_count, sub, columns).transpose(
            1, 0, 2, 3
        )
        returned_rows = lax.all_to_all(by_source, "expert", split_axis=0, concat_axis=0, tiled=True)
        all_slot_ids = member_ids * part + chunk * sub + within_ids
        weighted_place = jnp.where(
            (hit_arranged[:, :, None, None] == 1.0)
            & (prior_arranged[:, :, None, None] == all_slot_ids.astype(jnp.float32)),
            weight[:, :, None, None],
            0.0,
        ).reshape(tokens, expert_count * replica_count * sub)
        place_high = weighted_place.astype(jnp.bfloat16)
        place_low = (weighted_place - place_high.astype(jnp.float32)).astype(jnp.bfloat16)
        rows_flat = returned_rows.reshape(expert_count * replica_count * sub, columns)
        combined = (
            combined
            + jnp.dot(place_high, rows_flat, preferred_element_type=jnp.float32)
            + jnp.dot(place_low, rows_flat, preferred_element_type=jnp.float32)
        )
    arranged = combined.astype(jnp.bfloat16).reshape(replica_count, share_rows, step_count, columns)
    quarters = lax.all_to_all(arranged, "dp", split_axis=0, concat_axis=0, tiled=True)
    return quarters.transpose(1, 2, 0, 3).reshape(share_rows, step_count, model_width)


def solution(mesh):
    in_specs = (
        P("expert", None, None),
        P("expert", None, None),
        P("expert", None, None),
        P("expert"),
        P("expert"),
        P("expert"),
        P("expert", None, "dp"),
        P("expert", None, "dp"),
        P("expert", "dp", None),
    )
    out_specs = P(("dp", "expert"), None, None)
    return jax.shard_map(body, mesh=mesh, in_specs=in_specs, out_specs=out_specs, check_vma=False)
```

```python
import jax
import jax.numpy as jnp
from jax import lax
from jax.sharding import PartitionSpec as P

MOST_BASE = 16


def exchange_gather(matrix, replica, replica_count):
    width = matrix.shape[1] // replica_count
    pieces = [lax.dynamic_slice_in_dim(matrix, replica * width, width, axis=1)]
    for shift in range(1, replica_count):
        start = ((replica + shift) % replica_count) * width
        outgoing = lax.dynamic_slice_in_dim(matrix, start, width, axis=1)
        pairs = [(i, (i + shift) % replica_count) for i in range(replica_count)]
        pieces.append(lax.ppermute(outgoing, "dp", pairs))
    return jnp.stack(pieces, axis=0)


def exchange_all(block, replica_count):
    pieces = [block]
    for shift in range(1, replica_count):
        pairs = [(i, (i + shift) % replica_count) for i in range(replica_count)]
        pieces.append(lax.ppermute(block, "dp", pairs))
    return jnp.stack(pieces, axis=0)


def body(
    hidden_states, routes, route_weight, finish_step, group_keep, dest_slot, w_gate, w_up, w_down
):
    expert_count = lax.axis_size("expert")
    replica_count = lax.axis_size("dp")
    replica = lax.axis_index("dp")
    row_count, step_count, model_width = hidden_states.shape
    top_count = routes.shape[2]
    hidden_part = w_down.shape[1]
    columns = model_width // replica_count
    tokens = row_count * step_count
    slot_count = min(tokens, max(MOST_BASE, 2 * tokens * top_count // expert_count))
    slot_count = -(-slot_count // replica_count) * replica_count
    part = slot_count // replica_count
    by_member = lax.all_to_all(
        w_down[0].reshape(hidden_part, replica_count, columns),
        "dp",
        split_axis=1,
        concat_axis=0,
        tiled=True,
    ).reshape(replica_count, hidden_part, columns)
    down_cols = jnp.stack(
        [
            lax.dynamic_index_in_dim(
                by_member, (replica - shift) % replica_count, 0, keepdims=False
            )
            for shift in range(replica_count)
        ],
        axis=0,
    )
    step_ids = lax.broadcasted_iota(jnp.int32, (row_count, step_count), 1)
    live_mask = ((step_ids < finish_step[:, None]) & (group_keep[0] == 1)).reshape(tokens)
    gate_share = route_weight / jnp.sum(route_weight, axis=2, keepdims=True)
    expert_ids = lax.broadcasted_iota(jnp.int32, (1, 1, expert_count), 2)
    picked = (routes.reshape(tokens, top_count, 1) == expert_ids) & live_mask[:, None, None]
    hit_mask = jnp.sum(picked.astype(jnp.int32), axis=1)
    share_wide = jnp.broadcast_to(gate_share.reshape(tokens, top_count, 1), picked.shape)
    weight = jnp.sum(jnp.where(picked, share_wide, jnp.zeros_like(share_wide)), axis=1)
    prior_hits = jnp.cumsum(hit_mask, axis=0) - hit_mask
    flat_inputs = hidden_states.reshape(tokens, model_width)
    chunks = 2 if part % 2 == 0 else 1
    sub = part // chunks
    member_ids = lax.broadcasted_iota(jnp.int32, (1, 1, replica_count, 1), 2)
    within_ids = lax.broadcasted_iota(jnp.int32, (1, 1, 1, sub), 3)
    combined = jnp.zeros((tokens, columns), jnp.float32)
    for chunk in range(chunks):
        slot_ids = replica * part + chunk * sub + lax.broadcasted_iota(jnp.int32, (1, 1, sub), 2)
        placement = (hit_mask[:, :, None] == 1) & (prior_hits[:, :, None] == slot_ids)
        placement = placement.reshape(tokens, expert_count * sub)
        outgoing = lax.dot_general(
            placement.astype(jnp.bfloat16),
            flat_inputs,
            (((0,), (0,)), ((), ())),
            preferred_element_type=jnp.float32,
        ).astype(jnp.bfloat16)
        if chunk == 1:
            down_cols, outgoing = lax.optimization_barrier((down_cols, outgoing))
        arrived = lax.all_to_all(outgoing, "expert", split_axis=0, concat_axis=0, tiled=True)
        gathered = lax.all_gather(arrived, "dp", axis=0, tiled=True)
        gate_part = jnp.dot(gathered, w_gate[0], preferred_element_type=jnp.float32)
        up_part = jnp.dot(gathered, w_up[0], preferred_element_type=jnp.float32)
        activated = (jax.nn.silu(gate_part) * up_part).astype(jnp.bfloat16)
        hidden_all = exchange_all(activated, replica_count)
        expert_cols = lax.dot_general(
            hidden_all,
            down_cols,
            (((0, 2), (0, 1)), ((), ())),
            preferred_element_type=jnp.float32,
        ).astype(jnp.bfloat16)
        by_source = expert_cols.reshape(replica_count, expert_count, sub, columns).transpose(
            1, 0, 2, 3
        )
        returned_rows = lax.all_to_all(by_source, "expert", split_axis=0, concat_axis=0, tiled=True)
        all_slot_ids = member_ids * part + chunk * sub + within_ids
        weighted_place = jnp.where(
            (hit_mask[:, :, None, None] == 1) & (prior_hits[:, :, None, None] == all_slot_ids),
            weight[:, :, None, None],
            0.0,
        ).reshape(tokens, expert_count * replica_count * sub)
        combined = combined + jnp.dot(
            weighted_place,
            returned_rows.reshape(expert_count * replica_count * sub, columns).astype(jnp.float32),
            precision=lax.Precision.HIGHEST,
            preferred_element_type=jnp.float32,
        )
    share_rows = row_count // replica_count
    flat_device = dest_slot // share_rows
    target = flat_device // expert_count * share_rows + dest_slot % share_rows
    position_ids = lax.broadcasted_iota(jnp.int32, (replica_count * share_rows, row_count), 0)
    arrangement = (target[None, :] == position_ids).astype(jnp.float32)
    arranged = jnp.dot(
        arrangement,
        combined.reshape(row_count, step_count * columns),
        precision=lax.Precision.HIGHEST,
        preferred_element_type=jnp.float32,
    ).astype(jnp.bfloat16)
    arranged = arranged.reshape(replica_count, share_rows, step_count, columns)
    quarters = lax.all_to_all(arranged, "dp", split_axis=0, concat_axis=0, tiled=True)
    return quarters.transpose(1, 2, 0, 3).reshape(share_rows, step_count, model_width)


def solution(mesh):
    in_specs = (
        P("expert", None, None),
        P("expert", None, None),
        P("expert", None, None),
        P("expert"),
        P("expert"),
        P("expert"),
        P("expert", None, "dp"),
        P("expert", None, "dp"),
        P("expert", "dp", None),
    )
    out_specs = P(("dp", "expert"), None, None)
    return jax.shard_map(body, mesh=mesh, in_specs=in_specs, out_specs=out_specs, check_vma=False)
```

```python
import jax
import jax.numpy as jnp
from jax import lax
from jax.sharding import PartitionSpec as P

MOST_BASE = 16


def exchange_gather(matrix, replica, replica_count):
    width = matrix.shape[1] // replica_count
    pieces = [lax.dynamic_slice_in_dim(matrix, replica * width, width, axis=1)]
    for shift in range(1, replica_count):
        start = ((replica + shift) % replica_count) * width
        outgoing = lax.dynamic_slice_in_dim(matrix, start, width, axis=1)
        pairs = [(i, (i + shift) % replica_count) for i in range(replica_count)]
        pieces.append(lax.ppermute(outgoing, "dp", pairs))
    return pieces


def exchange_all(block, replica_count):
    pieces = [block]
    for shift in range(1, replica_count):
        pairs = [(i, (i + shift) % replica_count) for i in range(replica_count)]
        pieces.append(lax.ppermute(block, "dp", pairs))
    return jnp.stack(pieces, axis=0)


def body(
    hidden_states, routes, route_weight, finish_step, group_keep, dest_slot, w_gate, w_up, w_down
):
    expert_count = lax.axis_size("expert")
    replica_count = lax.axis_size("dp")
    replica = lax.axis_index("dp")
    row_count, step_count, model_width = hidden_states.shape
    top_count = routes.shape[2]
    hidden_part = w_down.shape[1]
    columns = model_width // replica_count
    tokens = row_count * step_count
    slot_count = min(tokens, max(MOST_BASE, 2 * tokens * top_count // expert_count))
    slot_count = -(-slot_count // replica_count) * replica_count
    part = slot_count // replica_count
    down_cols = exchange_gather(w_down[0], replica, replica_count)
    step_ids = lax.broadcasted_iota(jnp.int32, (row_count, step_count), 1)
    live_mask = ((step_ids < finish_step[:, None]) & (group_keep[0] == 1)).reshape(tokens)
    gate_share = route_weight / jnp.sum(route_weight, axis=2, keepdims=True)
    expert_ids = lax.broadcasted_iota(jnp.int32, (1, 1, expert_count), 2)
    picked = (routes.reshape(tokens, top_count, 1) == expert_ids) & live_mask[:, None, None]
    hit_mask = jnp.sum(picked.astype(jnp.int32), axis=1)
    share_wide = jnp.broadcast_to(gate_share.reshape(tokens, top_count, 1), picked.shape)
    weight = jnp.sum(jnp.where(picked, share_wide, jnp.zeros_like(share_wide)), axis=1)
    prior_hits = jnp.cumsum(hit_mask, axis=0) - hit_mask
    flat_inputs = hidden_states.reshape(tokens, model_width)
    chunks = 2 if part % 2 == 0 else 1
    sub = part // chunks
    member_ids = lax.broadcasted_iota(jnp.int32, (1, 1, replica_count, 1), 2)
    within_ids = lax.broadcasted_iota(jnp.int32, (1, 1, 1, sub), 3)
    combined = jnp.zeros((tokens, columns), jnp.float32)
    for chunk in range(chunks):
        slot_ids = replica * part + chunk * sub + lax.broadcasted_iota(jnp.int32, (1, 1, sub), 2)
        placement = (hit_mask[:, :, None] == 1) & (prior_hits[:, :, None] == slot_ids)
        placement = placement.reshape(tokens, expert_count * sub)
        outgoing = lax.dot_general(
            placement.astype(jnp.bfloat16),
            flat_inputs,
            (((0,), (0,)), ((), ())),
            preferred_element_type=jnp.float32,
        ).astype(jnp.bfloat16)
        if chunk == 1:
            down_cols, outgoing = lax.optimization_barrier((down_cols, outgoing))
        arrived = lax.all_to_all(outgoing, "expert", split_axis=0, concat_axis=0, tiled=True)
        gathered = lax.all_gather(arrived, "dp", axis=0, tiled=True)
        gate_part = jnp.dot(gathered, w_gate[0], preferred_element_type=jnp.float32)
        up_part = jnp.dot(gathered, w_up[0], preferred_element_type=jnp.float32)
        activated = (jax.nn.silu(gate_part) * up_part).astype(jnp.bfloat16)
        hidden_all = exchange_all(activated, replica_count)
        expert_cols = lax.dot_general(
            hidden_all,
            jnp.stack(down_cols, axis=0),
            (((0, 2), (0, 1)), ((), ())),
            preferred_element_type=jnp.float32,
        ).astype(jnp.bfloat16)
        by_source = expert_cols.reshape(replica_count, expert_count, sub, columns).transpose(
            1, 0, 2, 3
        )
        returned_rows = lax.all_to_all(by_source, "expert", split_axis=0, concat_axis=0, tiled=True)
        all_slot_ids = member_ids * part + chunk * sub + within_ids
        weighted_place = jnp.where(
            (hit_mask[:, :, None, None] == 1) & (prior_hits[:, :, None, None] == all_slot_ids),
            weight[:, :, None, None],
            0.0,
        ).reshape(tokens, expert_count * replica_count * sub)
        combined = combined + jnp.dot(
            weighted_place,
            returned_rows.reshape(expert_count * replica_count * sub, columns).astype(jnp.float32),
            precision=lax.Precision.HIGHEST,
            preferred_element_type=jnp.float32,
        )
    share_rows = row_count // replica_count
    flat_device = dest_slot // share_rows
    target = flat_device // expert_count * share_rows + dest_slot % share_rows
    position_ids = lax.broadcasted_iota(jnp.int32, (replica_count * share_rows, row_count), 0)
    arrangement = (target[None, :] == position_ids).astype(jnp.float32)
    arranged = jnp.dot(
        arrangement,
        combined.reshape(row_count, step_count * columns),
        precision=lax.Precision.HIGHEST,
        preferred_element_type=jnp.float32,
    ).astype(jnp.bfloat16)
    arranged = arranged.reshape(replica_count, share_rows, step_count, columns)
    quarters = lax.all_to_all(arranged, "dp", split_axis=0, concat_axis=0, tiled=True)
    return quarters.transpose(1, 2, 0, 3).reshape(share_rows, step_count, model_width)


def solution(mesh):
    in_specs = (
        P("expert", None, None),
        P("expert", None, None),
        P("expert", None, None),
        P("expert"),
        P("expert"),
        P("expert"),
        P("expert", None, "dp"),
        P("expert", None, "dp"),
        P("expert", "dp", None),
    )
    out_specs = P(("dp", "expert"), None, None)
    return jax.shard_map(body, mesh=mesh, in_specs=in_specs, out_specs=out_specs, check_vma=False)
```

```python
import jax
import jax.numpy as jnp
from jax import lax
from jax.sharding import PartitionSpec as P

MOST_BASE = 16


def exchange_gather(matrix, replica, replica_count):
    width = matrix.shape[1] // replica_count
    pieces = [lax.dynamic_slice_in_dim(matrix, replica * width, width, axis=1)]
    for shift in range(1, replica_count):
        start = ((replica + shift) % replica_count) * width
        outgoing = lax.dynamic_slice_in_dim(matrix, start, width, axis=1)
        pairs = [(i, (i + shift) % replica_count) for i in range(replica_count)]
        pieces.append(lax.ppermute(outgoing, "dp", pairs))
    return pieces


def exchange_all(block, replica_count):
    pieces = [block]
    for shift in range(1, replica_count):
        pairs = [(i, (i + shift) % replica_count) for i in range(replica_count)]
        pieces.append(lax.ppermute(block, "dp", pairs))
    return jnp.stack(pieces, axis=0)


def body(
    hidden_states, routes, route_weight, finish_step, group_keep, dest_slot, w_gate, w_up, w_down
):
    expert_count = lax.axis_size("expert")
    replica_count = lax.axis_size("dp")
    replica = lax.axis_index("dp")
    row_count, step_count, model_width = hidden_states.shape
    top_count = routes.shape[2]
    hidden_part = w_down.shape[1]
    columns = model_width // replica_count
    tokens = row_count * step_count
    slot_count = min(tokens, max(MOST_BASE, 2 * tokens * top_count // expert_count))
    slot_count = -(-slot_count // replica_count) * replica_count
    part = slot_count // replica_count
    down_cols = exchange_gather(w_down[0], replica, replica_count)
    step_ids = lax.broadcasted_iota(jnp.int32, (row_count, step_count), 1)
    live_mask = ((step_ids < finish_step[:, None]) & (group_keep[0] == 1)).reshape(tokens)
    gate_share = route_weight / jnp.sum(route_weight, axis=2, keepdims=True)
    expert_ids = lax.broadcasted_iota(jnp.int32, (1, 1, expert_count), 2)
    picked = (routes.reshape(tokens, top_count, 1) == expert_ids) & live_mask[:, None, None]
    hit_mask = jnp.sum(picked.astype(jnp.int32), axis=1)
    share_wide = jnp.broadcast_to(gate_share.reshape(tokens, top_count, 1), picked.shape)
    weight = jnp.sum(jnp.where(picked, share_wide, jnp.zeros_like(share_wide)), axis=1)
    prior_hits = jnp.cumsum(hit_mask, axis=0) - hit_mask
    flat_inputs = hidden_states.reshape(tokens, model_width)
    chunks = 2 if part % 2 == 0 else 1
    sub = part // chunks
    member_ids = lax.broadcasted_iota(jnp.int32, (1, 1, replica_count, 1), 2)
    within_ids = lax.broadcasted_iota(jnp.int32, (1, 1, 1, sub), 3)
    combined = jnp.zeros((tokens, columns), jnp.float32)
    for chunk in range(chunks):
        slot_ids = replica * part + chunk * sub + lax.broadcasted_iota(jnp.int32, (1, 1, sub), 2)
        placement = (hit_mask[:, :, None] == 1) & (prior_hits[:, :, None] == slot_ids)
        placement = placement.reshape(tokens, expert_count * sub)
        outgoing = lax.dot_general(
            placement.astype(jnp.bfloat16),
            flat_inputs,
            (((0,), (0,)), ((), ())),
            preferred_element_type=jnp.float32,
        ).astype(jnp.bfloat16)
        if chunk == 1:
            down_cols, outgoing = lax.optimization_barrier((down_cols, outgoing))
        arrived = lax.all_to_all(outgoing, "expert", split_axis=0, concat_axis=0, tiled=True)
        gathered = lax.all_gather(arrived, "dp", axis=0, tiled=True)
        gate_part = jnp.dot(gathered, w_gate[0], preferred_element_type=jnp.float32)
        up_part = jnp.dot(gathered, w_up[0], preferred_element_type=jnp.float32)
        activated = (jax.nn.silu(gate_part) * up_part).astype(jnp.bfloat16)
        hidden_all = exchange_all(activated, replica_count)
        expert_cols = lax.dot_general(
            hidden_all,
            jnp.stack(down_cols, axis=0),
            (((0, 2), (0, 1)), ((), ())),
            preferred_element_type=jnp.float32,
        ).astype(jnp.bfloat16)
        by_source = expert_cols.reshape(replica_count, expert_count, sub, columns).transpose(
            1, 0, 2, 3
        )
        returned_rows = lax.all_to_all(by_source, "expert", split_axis=0, concat_axis=0, tiled=True)
        all_slot_ids = member_ids * part + chunk * sub + within_ids
        weighted_place = jnp.where(
            (hit_mask[:, :, None, None] == 1) & (prior_hits[:, :, None, None] == all_slot_ids),
            weight[:, :, None, None],
            0.0,
        ).reshape(tokens, expert_count * replica_count * sub)
        combined = combined + jnp.dot(
            weighted_place,
            returned_rows.reshape(expert_count * replica_count * sub, columns).astype(jnp.float32),
            precision=lax.Precision.HIGHEST,
            preferred_element_type=jnp.float32,
        )
    share_rows = row_count // replica_count
    flat_device = dest_slot // share_rows
    target = flat_device // expert_count * share_rows + dest_slot % share_rows
    position_ids = lax.broadcasted_iota(jnp.int32, (replica_count * share_rows, row_count), 0)
    arrangement = (target[None, :] == position_ids).astype(jnp.bfloat16)
    arranged = jnp.dot(
        arrangement,
        combined.astype(jnp.bfloat16).reshape(row_count, step_count * columns),
        preferred_element_type=jnp.float32,
    ).astype(jnp.bfloat16)
    arranged = arranged.reshape(replica_count, share_rows, step_count, columns)
    quarters = lax.all_to_all(arranged, "dp", split_axis=0, concat_axis=0, tiled=True)
    return quarters.transpose(1, 2, 0, 3).reshape(share_rows, step_count, model_width)


def solution(mesh):
    in_specs = (
        P("expert", None, None),
        P("expert", None, None),
        P("expert", None, None),
        P("expert"),
        P("expert"),
        P("expert"),
        P("expert", None, "dp"),
        P("expert", None, "dp"),
        P("expert", "dp", None),
    )
    out_specs = P(("dp", "expert"), None, None)
    return jax.shard_map(body, mesh=mesh, in_specs=in_specs, out_specs=out_specs, check_vma=False)
```

```python
import jax
import jax.numpy as jnp
from jax import lax
from jax.sharding import PartitionSpec as P

MOST_BASE = 16


def exchange_gather(matrix, replica, replica_count):
    width = matrix.shape[1] // replica_count
    pieces = [lax.dynamic_slice_in_dim(matrix, replica * width, width, axis=1)]
    for shift in range(1, replica_count):
        start = ((replica + shift) % replica_count) * width
        outgoing = lax.dynamic_slice_in_dim(matrix, start, width, axis=1)
        pairs = [(i, (i + shift) % replica_count) for i in range(replica_count)]
        pieces.append(lax.ppermute(outgoing, "dp", pairs))
    return pieces


def exchange_all(block, replica_count):
    pieces = [block]
    for shift in range(1, replica_count):
        pairs = [(i, (i + shift) % replica_count) for i in range(replica_count)]
        pieces.append(lax.ppermute(block, "dp", pairs))
    return jnp.stack(pieces, axis=0)


def body(
    hidden_states, routes, route_weight, finish_step, group_keep, dest_slot, w_gate, w_up, w_down
):
    expert_count = lax.axis_size("expert")
    replica_count = lax.axis_size("dp")
    replica = lax.axis_index("dp")
    row_count, step_count, model_width = hidden_states.shape
    top_count = routes.shape[2]
    hidden_part = w_down.shape[1]
    columns = model_width // replica_count
    tokens = row_count * step_count
    slot_count = min(tokens, max(MOST_BASE, 2 * tokens * top_count // expert_count))
    slot_count = -(-slot_count // replica_count) * replica_count
    part = slot_count // replica_count
    down_cols = exchange_gather(w_down[0], replica, replica_count)
    step_ids = lax.broadcasted_iota(jnp.int32, (row_count, step_count), 1)
    live_mask = ((step_ids < finish_step[:, None]) & (group_keep[0] == 1)).reshape(tokens)
    gate_share = route_weight / jnp.sum(route_weight, axis=2, keepdims=True)
    expert_ids = lax.broadcasted_iota(jnp.int32, (1, 1, expert_count), 2)
    picked = (routes.reshape(tokens, top_count, 1) == expert_ids) & live_mask[:, None, None]
    hit_mask = jnp.sum(picked.astype(jnp.int32), axis=1)
    share_wide = jnp.broadcast_to(gate_share.reshape(tokens, top_count, 1), picked.shape)
    weight = jnp.sum(jnp.where(picked, share_wide, jnp.zeros_like(share_wide)), axis=1)
    prior_hits = jnp.cumsum(hit_mask, axis=0) - hit_mask
    flat_inputs = hidden_states.reshape(tokens, model_width)
    chunks = 2 if part % 2 == 0 else 1
    sub = part // chunks
    member_ids = lax.broadcasted_iota(jnp.int32, (1, 1, replica_count, 1), 2)
    within_ids = lax.broadcasted_iota(jnp.int32, (1, 1, 1, sub), 3)
    combined = jnp.zeros((tokens, columns), jnp.float32)
    outgoings = []
    for chunk in range(chunks):
        slot_ids = replica * part + chunk * sub + lax.broadcasted_iota(jnp.int32, (1, 1, sub), 2)
        placement = (hit_mask[:, :, None] == 1) & (prior_hits[:, :, None] == slot_ids)
        placement = placement.reshape(tokens, expert_count * sub)
        outgoings.append(
            lax.dot_general(
                placement.astype(jnp.bfloat16),
                flat_inputs,
                (((0,), (0,)), ((), ())),
                preferred_element_type=jnp.float32,
            ).astype(jnp.bfloat16)
        )
    if chunks > 1:
        down_cols, outgoings[1] = lax.optimization_barrier((down_cols, outgoings[1]))
    down_stack = jnp.stack(down_cols, axis=0)
    for chunk in range(chunks):
        outgoing = outgoings[chunk]
        arrived = lax.all_to_all(outgoing, "expert", split_axis=0, concat_axis=0, tiled=True)
        gathered = lax.all_gather(arrived, "dp", axis=0, tiled=True)
        gate_part = jnp.dot(gathered, w_gate[0], preferred_element_type=jnp.float32)
        up_part = jnp.dot(gathered, w_up[0], preferred_element_type=jnp.float32)
        activated = (jax.nn.silu(gate_part) * up_part).astype(jnp.bfloat16)
        hidden_all = exchange_all(activated, replica_count)
        expert_cols = lax.dot_general(
            hidden_all,
            down_stack,
            (((0, 2), (0, 1)), ((), ())),
            preferred_element_type=jnp.float32,
        ).astype(jnp.bfloat16)
        by_source = expert_cols.reshape(replica_count, expert_count, sub, columns).transpose(
            1, 0, 2, 3
        )
        returned_rows = lax.all_to_all(by_source, "expert", split_axis=0, concat_axis=0, tiled=True)
        all_slot_ids = member_ids * part + chunk * sub + within_ids
        weighted_place = jnp.where(
            (hit_mask[:, :, None, None] == 1) & (prior_hits[:, :, None, None] == all_slot_ids),
            weight[:, :, None, None],
            0.0,
        ).reshape(tokens, expert_count * replica_count * sub)
        combined = combined + jnp.dot(
            weighted_place,
            returned_rows.reshape(expert_count * replica_count * sub, columns).astype(jnp.float32),
            precision=lax.Precision.HIGHEST,
            preferred_element_type=jnp.float32,
        )
    share_rows = row_count // replica_count
    flat_device = dest_slot // share_rows
    target = flat_device // expert_count * share_rows + dest_slot % share_rows
    position_ids = lax.broadcasted_iota(jnp.int32, (replica_count * share_rows, row_count), 0)
    arrangement = (target[None, :] == position_ids).astype(jnp.bfloat16)
    arranged = jnp.dot(
        arrangement,
        combined.astype(jnp.bfloat16).reshape(row_count, step_count * columns),
        preferred_element_type=jnp.float32,
    ).astype(jnp.bfloat16)
    arranged = arranged.reshape(replica_count, share_rows, step_count, columns)
    quarters = lax.all_to_all(arranged, "dp", split_axis=0, concat_axis=0, tiled=True)
    return quarters.transpose(1, 2, 0, 3).reshape(share_rows, step_count, model_width)


def solution(mesh):
    in_specs = (
        P("expert", None, None),
        P("expert", None, None),
        P("expert", None, None),
        P("expert"),
        P("expert"),
        P("expert"),
        P("expert", None, "dp"),
        P("expert", None, "dp"),
        P("expert", "dp", None),
    )
    out_specs = P(("dp", "expert"), None, None)
    return jax.shard_map(body, mesh=mesh, in_specs=in_specs, out_specs=out_specs, check_vma=False)
```

```python
import jax
import jax.numpy as jnp
from jax import lax
from jax.sharding import PartitionSpec as P

MOST_BASE = 16


def exchange_gather(matrix, replica, replica_count):
    width = matrix.shape[1] // replica_count
    pieces = [lax.dynamic_slice_in_dim(matrix, replica * width, width, axis=1)]
    for shift in range(1, replica_count):
        start = ((replica + shift) % replica_count) * width
        outgoing = lax.dynamic_slice_in_dim(matrix, start, width, axis=1)
        pairs = [(i, (i + shift) % replica_count) for i in range(replica_count)]
        pieces.append(lax.ppermute(outgoing, "dp", pairs))
    return pieces


def exchange_all(block, replica_count):
    pieces = [block]
    for shift in range(1, replica_count):
        pairs = [(i, (i + shift) % replica_count) for i in range(replica_count)]
        pieces.append(lax.ppermute(block, "dp", pairs))
    return jnp.stack(pieces, axis=0)


def body(
    hidden_states, routes, route_weight, finish_step, group_keep, dest_slot, w_gate, w_up, w_down
):
    expert_count = lax.axis_size("expert")
    replica_count = lax.axis_size("dp")
    replica = lax.axis_index("dp")
    row_count, step_count, model_width = hidden_states.shape
    top_count = routes.shape[2]
    hidden_part = w_down.shape[1]
    columns = model_width // replica_count
    tokens = row_count * step_count
    slot_count = min(tokens, max(MOST_BASE, 2 * tokens * top_count // expert_count))
    slot_count = -(-slot_count // replica_count) * replica_count
    part = slot_count // replica_count
    down_cols = exchange_gather(w_down[0], replica, replica_count)
    step_ids = lax.broadcasted_iota(jnp.int32, (row_count, step_count), 1)
    live_mask = ((step_ids < finish_step[:, None]) & (group_keep[0] == 1)).reshape(tokens)
    gate_share = route_weight / jnp.sum(route_weight, axis=2, keepdims=True)
    expert_ids = lax.broadcasted_iota(jnp.int32, (1, 1, expert_count), 2)
    picked = (routes.reshape(tokens, top_count, 1) == expert_ids) & live_mask[:, None, None]
    hit_mask = jnp.sum(picked.astype(jnp.int32), axis=1)
    share_wide = jnp.broadcast_to(gate_share.reshape(tokens, top_count, 1), picked.shape)
    weight = jnp.sum(jnp.where(picked, share_wide, jnp.zeros_like(share_wide)), axis=1)
    prior_hits = jnp.cumsum(hit_mask, axis=0) - hit_mask
    flat_inputs = hidden_states.reshape(tokens, model_width)
    chunks = 2 if part % 2 == 0 else 1
    sub = part // chunks
    member_ids = lax.broadcasted_iota(jnp.int32, (1, 1, replica_count, 1), 2)
    within_ids = lax.broadcasted_iota(jnp.int32, (1, 1, 1, sub), 3)
    combined = jnp.zeros((tokens, columns), jnp.float32)
    outgoings = []
    for chunk in range(chunks):
        slot_ids = replica * part + chunk * sub + lax.broadcasted_iota(jnp.int32, (1, 1, sub), 2)
        placement = (hit_mask[:, :, None] == 1) & (prior_hits[:, :, None] == slot_ids)
        placement = placement.reshape(tokens, expert_count * sub)
        outgoings.append(
            lax.dot_general(
                placement.astype(jnp.bfloat16),
                flat_inputs,
                (((0,), (0,)), ((), ())),
                preferred_element_type=jnp.float32,
            ).astype(jnp.bfloat16)
        )
    if chunks > 1:
        down_cols, outgoings[1] = lax.optimization_barrier((down_cols, outgoings[1]))
    down_stack = jnp.stack(down_cols, axis=0)
    for chunk in range(chunks):
        outgoing = outgoings[chunk]
        arrived = lax.all_to_all(outgoing, "expert", split_axis=0, concat_axis=0, tiled=True)
        gathered = lax.all_gather(arrived, "dp", axis=0, tiled=True)
        gate_part = jnp.dot(gathered, w_gate[0], preferred_element_type=jnp.float32)
        up_part = jnp.dot(gathered, w_up[0], preferred_element_type=jnp.float32)
        activated = (jax.nn.silu(gate_part) * up_part).astype(jnp.bfloat16)
        hidden_all = exchange_all(activated, replica_count)
        expert_cols = lax.dot_general(
            hidden_all,
            down_stack,
            (((0, 2), (0, 1)), ((), ())),
            preferred_element_type=jnp.float32,
        ).astype(jnp.bfloat16)
        by_source = expert_cols.reshape(replica_count, expert_count, sub, columns).transpose(
            1, 0, 2, 3
        )
        returned_rows = lax.all_to_all(by_source, "expert", split_axis=0, concat_axis=0, tiled=True)
        all_slot_ids = member_ids * part + chunk * sub + within_ids
        weighted_place = jnp.where(
            (hit_mask[:, :, None, None] == 1) & (prior_hits[:, :, None, None] == all_slot_ids),
            weight[:, :, None, None],
            0.0,
        ).reshape(tokens, expert_count * replica_count * sub)
        combined = combined + jnp.dot(
            weighted_place,
            returned_rows.reshape(expert_count * replica_count * sub, columns).astype(jnp.float32),
            precision=lax.Precision.HIGH,
            preferred_element_type=jnp.float32,
        )
    share_rows = row_count // replica_count
    flat_device = dest_slot // share_rows
    target = flat_device // expert_count * share_rows + dest_slot % share_rows
    position_ids = lax.broadcasted_iota(jnp.int32, (replica_count * share_rows, row_count), 0)
    arrangement = (target[None, :] == position_ids).astype(jnp.bfloat16)
    arranged = jnp.dot(
        arrangement,
        combined.astype(jnp.bfloat16).reshape(row_count, step_count * columns),
        preferred_element_type=jnp.float32,
    ).astype(jnp.bfloat16)
    arranged = arranged.reshape(replica_count, share_rows, step_count, columns)
    quarters = lax.all_to_all(arranged, "dp", split_axis=0, concat_axis=0, tiled=True)
    return quarters.transpose(1, 2, 0, 3).reshape(share_rows, step_count, model_width)


def solution(mesh):
    in_specs = (
        P("expert", None, None),
        P("expert", None, None),
        P("expert", None, None),
        P("expert"),
        P("expert"),
        P("expert"),
        P("expert", None, "dp"),
        P("expert", None, "dp"),
        P("expert", "dp", None),
    )
    out_specs = P(("dp", "expert"), None, None)
    return jax.shard_map(body, mesh=mesh, in_specs=in_specs, out_specs=out_specs, check_vma=False)
```

```python
import jax
import jax.numpy as jnp
from jax import lax
from jax.sharding import PartitionSpec as P

MOST_BASE = 16


def exchange_gather(matrix, replica, replica_count):
    width = matrix.shape[1] // replica_count
    pieces = [lax.dynamic_slice_in_dim(matrix, replica * width, width, axis=1)]
    for shift in range(1, replica_count):
        start = ((replica + shift) % replica_count) * width
        outgoing = lax.dynamic_slice_in_dim(matrix, start, width, axis=1)
        pairs = [(i, (i + shift) % replica_count) for i in range(replica_count)]
        pieces.append(lax.ppermute(outgoing, "dp", pairs))
    return pieces


def exchange_all(block, replica_count):
    pieces = [block]
    for shift in range(1, replica_count):
        pairs = [(i, (i + shift) % replica_count) for i in range(replica_count)]
        pieces.append(lax.ppermute(block, "dp", pairs))
    return jnp.stack(pieces, axis=0)


def body(
    hidden_states, routes, route_weight, finish_step, group_keep, dest_slot, w_gate, w_up, w_down
):
    expert_count = lax.axis_size("expert")
    replica_count = lax.axis_size("dp")
    replica = lax.axis_index("dp")
    row_count, step_count, model_width = hidden_states.shape
    top_count = routes.shape[2]
    hidden_part = w_down.shape[1]
    columns = model_width // replica_count
    tokens = row_count * step_count
    slot_count = min(tokens, max(MOST_BASE, 2 * tokens * top_count // expert_count))
    slot_count = -(-slot_count // replica_count) * replica_count
    part = slot_count // replica_count
    down_cols = exchange_gather(w_down[0], replica, replica_count)
    step_ids = lax.broadcasted_iota(jnp.int32, (row_count, step_count), 1)
    live_mask = ((step_ids < finish_step[:, None]) & (group_keep[0] == 1)).reshape(tokens)
    gate_share = route_weight / jnp.sum(route_weight, axis=2, keepdims=True)
    expert_ids = lax.broadcasted_iota(jnp.int32, (1, 1, expert_count), 2)
    picked = (routes.reshape(tokens, top_count, 1) == expert_ids) & live_mask[:, None, None]
    hit_mask = jnp.sum(picked.astype(jnp.int32), axis=1)
    share_wide = jnp.broadcast_to(gate_share.reshape(tokens, top_count, 1), picked.shape)
    weight = jnp.sum(jnp.where(picked, share_wide, jnp.zeros_like(share_wide)), axis=1)
    prior_hits = jnp.cumsum(hit_mask, axis=0) - hit_mask
    flat_inputs = hidden_states.reshape(tokens, model_width)
    chunks = 2 if part % 2 == 0 else 1
    sub = part // chunks
    member_ids = lax.broadcasted_iota(jnp.int32, (1, 1, replica_count, 1), 2)
    within_ids = lax.broadcasted_iota(jnp.int32, (1, 1, 1, sub), 3)
    combined = jnp.zeros((tokens, columns), jnp.float32)
    outgoings = []
    for chunk in range(chunks):
        slot_ids = replica * part + chunk * sub + lax.broadcasted_iota(jnp.int32, (1, 1, sub), 2)
        placement = (hit_mask[:, :, None] == 1) & (prior_hits[:, :, None] == slot_ids)
        placement = placement.reshape(tokens, expert_count * sub)
        outgoings.append(
            lax.dot_general(
                placement.astype(jnp.bfloat16),
                flat_inputs,
                (((0,), (0,)), ((), ())),
                preferred_element_type=jnp.float32,
            ).astype(jnp.bfloat16)
        )
    if chunks > 1:
        down_cols, outgoings[1] = lax.optimization_barrier((down_cols, outgoings[1]))
    down_stack = jnp.stack(down_cols, axis=0)
    for chunk in range(chunks):
        outgoing = outgoings[chunk]
        arrived = lax.all_to_all(outgoing, "expert", split_axis=0, concat_axis=0, tiled=True)
        gathered = lax.all_gather(arrived, "dp", axis=0, tiled=True)
        gate_part = jnp.dot(gathered, w_gate[0], preferred_element_type=jnp.float32)
        up_part = jnp.dot(gathered, w_up[0], preferred_element_type=jnp.float32)
        activated = (jax.nn.silu(gate_part) * up_part).astype(jnp.bfloat16)
        hidden_all = exchange_all(activated, replica_count)
        expert_cols = lax.dot_general(
            hidden_all,
            down_stack,
            (((0, 2), (0, 1)), ((), ())),
            preferred_element_type=jnp.float32,
        ).astype(jnp.bfloat16)
        by_source = expert_cols.reshape(replica_count, expert_count, sub, columns).transpose(
            1, 0, 2, 3
        )
        returned_rows = lax.all_to_all(by_source, "expert", split_axis=0, concat_axis=0, tiled=True)
        all_slot_ids = member_ids * part + chunk * sub + within_ids
        weighted_place = jnp.where(
            (hit_mask[:, :, None, None] == 1) & (prior_hits[:, :, None, None] == all_slot_ids),
            weight[:, :, None, None],
            0.0,
        ).reshape(tokens, expert_count * replica_count * sub)
        combined = combined + jnp.dot(
            weighted_place,
            returned_rows.reshape(expert_count * replica_count * sub, columns).astype(jnp.float32),
            precision=lax.Precision.HIGHEST,
            preferred_element_type=jnp.float32,
        )
    share_rows = row_count // replica_count
    flat_device = dest_slot // share_rows
    target = flat_device // expert_count * share_rows + dest_slot % share_rows
    position_ids = lax.broadcasted_iota(jnp.int32, (replica_count * share_rows, row_count), 0)
    arrangement = (target[None, :] == position_ids).astype(jnp.bfloat16)
    arranged = jnp.dot(
        arrangement,
        combined.astype(jnp.bfloat16).reshape(row_count, step_count * columns),
        preferred_element_type=jnp.float32,
    ).astype(jnp.bfloat16)
    arranged = arranged.reshape(replica_count, share_rows, step_count, columns)
    quarters = lax.all_to_all(arranged, "dp", split_axis=0, concat_axis=3, tiled=True)
    return quarters.reshape(share_rows, step_count, model_width)


def solution(mesh):
    in_specs = (
        P("expert", None, None),
        P("expert", None, None),
        P("expert", None, None),
        P("expert"),
        P("expert"),
        P("expert"),
        P("expert", None, "dp"),
        P("expert", None, "dp"),
        P("expert", "dp", None),
    )
    out_specs = P(("dp", "expert"), None, None)
    return jax.shard_map(body, mesh=mesh, in_specs=in_specs, out_specs=out_specs, check_vma=False)
```
